128 devices in a mesh: gx: 4 (over z_lo, core), gy: 4 (over x), gz: 8 (over z_hi, y).
Axes of the slice: x: 4, y: 4, z: 4 (z_hi: 2, z_lo: 2; z = z_hi * 2 + z_lo), core: 2. Of those that a mesh axis runs over, the one named last changes fastest.
Arguments:
- coefficients: bfloat16 [8, 16, 16, 512, 128], P('gx', 'gy', 'gz'), may hold values from -6 to 6
- level_weights: bfloat16 [4, 2, 2, 512, 512], replicated, may hold values from -0.125 to 0.125
- coupling: bfloat16 [6, 512, 512], replicated, may hold values from -0.109375 to 0.109375
- positions: float32 [3, 1048576], P(None, ('gx', 'gy', 'gz')), may hold values from -1 to 1
- block_leaf: int32 [8192], P(('gx', 'gy', 'gz')), may hold values from 0 to 15
- block_count: int32 [8192], P(('gx', 'gy', 'gz')), may hold values from 1 to 128
Outputs:
- samples: bfloat16 [1048576, 128], P(('gx', 'gy', 'gz'))
The draws below stay inside these ranges and needn't reach their ends.
Inputs may be any that keep to these rules, and one draw needn't show every extreme that they name: `block_leaf`: each block names one of the 16 leaves of the device that holds the block.
All inputs are finite; a program needn't handle non-finite values.
Results may differ from the reference program's by a relative error of at most 0.015.
Values may be sent and summed in bfloat16 or wider, within the bound.
No kernel may reach another device: no remote copies, remote signals or barrier semaphores. Data moves between devices by JAX's collectives and lax.ppermute only.
A program may use at most 128 MiB of HBM per device.

```python
import math
import jax
import jax.numpy as jnp
import numpy as np
from jax import lax

PTS = 8
ROWS = 128
LEVELS = 4
LX = 2
LY = 4
LZ = 2
BLK_DEV = 64
CHEB = 512
COLS = 128
LB = 16
NLX = 8
NLY = 16
NLZ = 16
NBLK = 8192
NSAMP = 1048576
N_GX = 4
N_GY = 4
N_GZ = 8


def touch_ends(values, key, least, top_value):
    index_at = [jax.random.randint(jax.random.fold_in(key, axis), (), 0, length) for axis, length in enumerate(values.shape)]
    longest = values.shape.index(max(values.shape))
    next_to = index_at[:longest] + [(index_at[longest] + 1) % values.shape[longest]] + index_at[longest + 1:]
    return values.at[tuple(index_at)].set(least).at[tuple(next_to)].set(top_value)


def level_of(key, shape, split, low, largest):
    level, own = 1.0, jax.random.fold_in(key, 6)
    for dim, blocks in split:
        steps = jnp.exp(jax.random.uniform(jax.random.fold_in(own, dim), (blocks,), jnp.float32, low / len(split), largest / len(split)))
        level = level * jnp.repeat(steps, shape[dim] // blocks).reshape([-1 if axis == dim else 1 for axis in range(len(shape))])
    return level


def rank_table(number_of, skew):
    weights = [(1 << 20) // math.isqrt(grade ** skew) + 1 for grade in range(1, number_of + 1)]
    deviation = 1 + sum(weights) // (1 << 30)
    return np.cumsum(np.array([max(1, weight // deviation) for weight in weights]))


def ranked_ids(stream_key, shape, amount, slope):
    table = rank_table(amount, slope)
    lot = jax.random.randint(jax.random.fold_in(stream_key, 1), shape, 0, int(table[amount - 1]))
    standing = jnp.searchsorted(jnp.asarray(table, jnp.int32), lot, side="right")
    return jax.random.permutation(jax.random.fold_in(stream_key, 2), amount)[standing].astype(jnp.int32)


def centred(stream_key, dims, scale, reach, shards=(), held_as=jnp.bfloat16):
    array = jax.random.normal(stream_key, dims, jnp.float32) * scale
    if len(shards) > 0:
        array = level_of(stream_key, dims, shards, -0.22, 0.18) * array
    return jnp.clip(array, min=-reach, max=reach).astype(held_as)


def setup_inputs(seed: int = 0) -> dict:
    arg_keys = jax.random.split(jax.random.key(seed), 7)
    return {
        "coefficients": centred(arg_keys[0], (NLX, NLY, NLZ, CHEB, COLS), 1.0, 6.0, ((0, 4), (1, 4), (2, 8))),
        "level_weights": centred(arg_keys[1], (LEVELS, 2, 2, CHEB, CHEB), (4 * CHEB) ** -0.5, 0.125),
        "coupling": centred(arg_keys[2], (6, CHEB, CHEB), (6 * CHEB) ** -0.5, 0.109375),
        "positions": jnp.clip(jax.random.uniform(arg_keys[3], (3, NSAMP), jnp.float32, -1.0, 1.0) * level_of(arg_keys[3], (3, NSAMP), ((1, 128),), -0.4, 0.0), -1.0, 1.0),
        "block_leaf": touch_ends(ranked_ids(arg_keys[4], (NBLK,), LB, 2), jax.random.fold_in(arg_keys[4], 3), 0, LB - 1).astype(jnp.int32),
        "block_count": touch_ends(jax.random.randint(arg_keys[5], (NBLK,), 1, ROWS + 1), jax.random.fold_in(arg_keys[5], 1), 1, ROWS).astype(jnp.int32),
    }


def swapped(block):
    half = block.shape[-1] // 2
    return jnp.concatenate([-block[..., half:], block[..., :half]], axis=-1)


def flipped(block, dim, count, bit):
    shape = block.shape
    width = 1 << bit
    inner = shape[dim] // count * width
    grouped = block.reshape(shape[:dim] + (count // (2 * width), 2, inner) + shape[dim + 1:])
    return jnp.flip(grouped, axis=dim + 1).reshape(shape)


def apply_map(weights, block):
    return jnp.einsum("jk,...kc->...jc", weights.astype(jnp.float32), block.astype(jnp.float32))


def mix(block, other, weights):
    total = apply_map(weights[0, 0], block) + apply_map(weights[0, 1], swapped(block))
    total = total + apply_map(weights[1, 0], other) + apply_map(weights[1, 1], swapped(other))
    return total.astype(jnp.bfloat16)


def lagrange(coords, points):
    nodes = jnp.cos(math.pi * (2.0 * jnp.arange(points, dtype=jnp.float32) + 1.0) / (2.0 * points))
    basis = []
    for j in range(points):
        term = jnp.ones_like(coords)
        for m in range(points):
            if m != j:
                term = term * (coords - nodes[m]) / (nodes[j] - nodes[m])
        basis.append(term)
    return jnp.stack(basis, axis=-1)


def sample_weights(coords, points):
    along_x = lagrange(coords[0], points)
    along_y = lagrange(coords[1], points)
    along_z = lagrange(coords[2], points)
    prod = along_x[..., :, None, None] * along_y[..., None, :, None] * along_z[..., None, None, :]
    return prod.reshape(coords.shape[1:] + (points ** 3,)).astype(jnp.bfloat16)


def reference(coefficients, level_weights, coupling, positions, block_leaf, block_count):
    current = coefficients
    plan = ((0, N_GX, 0), (0, N_GX, 1), (1, N_GY, 0), (2, N_GZ, 0))
    for level in range(4):
        dim, count, bit = plan[level]
        other = flipped(current, dim, count, bit)
        current = mix(current, other, level_weights[level])
    padded = jnp.pad(current, ((1, 1), (1, 1), (1, 1), (0, 0), (0, 0)))
    neighbours = (padded[:-2, 1:-1, 1:-1], padded[2:, 1:-1, 1:-1], padded[1:-1, :-2, 1:-1],
                  padded[1:-1, 2:, 1:-1], padded[1:-1, 1:-1, :-2], padded[1:-1, 1:-1, 2:])
    total = current.astype(jnp.float32)
    for index in range(6):
        total = total + apply_map(coupling[index], neighbours[index])
    grid = total.astype(jnp.bfloat16)
    cheb = grid.shape[3]
    cols = grid.shape[4]
    devices = N_GX * N_GY * N_GZ
    per_device = grid.reshape(N_GX, LX, N_GY, LY, N_GZ, LZ, cheb, cols)
    per_device = per_device.transpose(0, 2, 4, 1, 3, 5, 6, 7).reshape(devices, LX * LY * LZ, cheb, cols)
    coords = positions.reshape(3, devices, BLK_DEV, ROWS).transpose(1, 0, 2, 3)
    leaves = block_leaf.reshape(devices, BLK_DEV)
    counts = block_count.reshape(devices, BLK_DEV)

    def one_device(items):
        leaf_grid, coord, leaf, count = items
        weights = sample_weights(coord, PTS)
        blocks = jnp.take(leaf_grid, leaf, axis=0)
        values = jnp.einsum("brk,bkc->brc", weights.astype(jnp.float32), blocks.astype(jnp.float32))
        live = jnp.arange(ROWS, dtype=jnp.int32)[None, :] < count[:, None]
        values = jnp.where(live[:, :, None], values, jnp.float32(0.0))
        return values.reshape(BLK_DEV * ROWS, cols).astype(jnp.bfloat16)

    result = lax.map(one_device, (per_device, coords, leaves, counts))
    return result.reshape(devices * BLK_DEV * ROWS, cols)
```

```python
import math

import numpy as np
import jax
import jax.numpy as jnp
from jax import lax
from jax.experimental import pallas as pl
from jax.experimental.pallas import tpu as pltpu
from jax.sharding import PartitionSpec as P

PTS = 8
ROWS = 128
BLOCKS_PER_STEP = 8

NODES = [
    float(v)
    for v in np.cos(
        np.float32(math.pi) * (np.float32(2.0) * np.arange(PTS, dtype=np.float32) + np.float32(1.0)) / np.float32(2.0 * PTS)
    ).astype(np.float32)
]


def from_partner(shard, axis, apart):
    return lax.ppermute(shard, axis, [(i, i ^ 1 << apart) for i in range(lax.axis_size(axis))])


def extended(cells, sides, width):
    for axis, dim in sides:
        count = lax.axis_size(axis)
        ends = count - 1
        head = lax.slice_in_dim(cells, 0, width, axis=dim)
        tail = lax.slice_in_dim(cells, cells.shape[dim] - width, cells.shape[dim], axis=dim)
        cells = jnp.concatenate(
            [
                lax.ppermute(tail, axis, [(i, (i + 1) % count) for i in range(ends)]),
                cells,
                lax.ppermute(head, axis, [((i + 1) % count, i) for i in range(ends)]),
            ],
            axis=dim,
        )
    return cells


def swapped(block):
    half = block.shape[-1] // 2
    return jnp.concatenate([-block[..., half:], block[..., :half]], axis=-1)


def apply_map(weights, block):
    return jnp.einsum("jk,...kc->...jc", weights, block, preferred_element_type=jnp.float32)


def mix(block, other, weights):
    total = apply_map(weights[0, 0], block) + apply_map(weights[0, 1], swapped(block))
    total = total + apply_map(weights[1, 0], other) + apply_map(weights[1, 1], swapped(other))
    return total.astype(jnp.bfloat16)


def basis(u, row):
    ub = jnp.broadcast_to(u, (PTS, ROWS))
    tcol = jnp.zeros((PTS, ROWS), jnp.float32)
    for j in range(PTS):
        tcol = jnp.where(row == j, NODES[j], tcol)
    term = jnp.ones((PTS, ROWS), jnp.float32)
    for m in range(PTS):
        own = row == m
        num = jnp.where(own, 1.0, ub - NODES[m])
        den = jnp.where(own, 1.0, tcol - NODES[m])
        term = term * num / den
    return term


def sample_kernel(leaf_ref, count_ref, pos_ref, grid_ref, out_ref):
    step = pl.program_id(0)
    row = lax.broadcasted_iota(jnp.int32, (PTS, ROWS), 0)
    live_row = lax.broadcasted_iota(jnp.int32, (ROWS, out_ref.shape[1]), 0)
    for i in range(BLOCKS_PER_STEP):
        b = step * BLOCKS_PER_STEP + i
        u = pos_ref[:, i * ROWS:(i + 1) * ROWS]
        lx = basis(u[0:1, :], row)
        ly = basis(u[1:2, :], row)
        lz = basis(u[2:3, :], row)
        pieces = []
        for jx in range(PTS):
            bx = jnp.broadcast_to(lx[jx:jx + 1, :], (PTS, ROWS))
            for jy in range(PTS):
                by = jnp.broadcast_to(ly[jy:jy + 1, :], (PTS, ROWS))
                pieces.append((bx * by) * lz)
        weights_t = jnp.concatenate(pieces, axis=0).astype(jnp.bfloat16)
        leaf = grid_ref[leaf_ref[b]]
        values = lax.dot_general(
            weights_t, leaf, (((0,), (0,)), ((), ())), preferred_element_type=jnp.float32
        )
        values = jnp.where(live_row < count_ref[b], values, 0.0)
        out_ref[i * ROWS:(i + 1) * ROWS, :] = values.astype(out_ref.dtype)


def sample(leaf_grid, positions, block_leaf, block_count):
    leaves, cheb, cols = leaf_grid.shape
    blocks = block_leaf.shape[0]
    width = BLOCKS_PER_STEP * ROWS
    spec = pltpu.PrefetchScalarGridSpec(
        num_scalar_prefetch=2,
        grid=(blocks // BLOCKS_PER_STEP,),
        in_specs=[
            pl.BlockSpec((3, width), lambda s, lf, ct: (0, s)),
            pl.BlockSpec((leaves, cheb, cols), lambda s, lf, ct: (0, 0, 0)),
        ],
        out_specs=pl.BlockSpec((width, cols), lambda s, lf, ct: (s, 0)),
    )
    return pl.pallas_call(
        sample_kernel,
        grid_spec=spec,
        out_shape=jax.ShapeDtypeStruct((blocks * ROWS, cols), jnp.bfloat16),
    )(block_leaf, block_count, positions, leaf_grid)


def local(coefficients, level_weights, coupling, positions, block_leaf, block_count):
    current = coefficients
    for level in range(2):
        other = from_partner(current, "gx", level)
        current = mix(current, other, level_weights[level])
    other = from_partner(current, "gy", 0)
    current = mix(current, other, level_weights[2])
    other = from_partner(current, "gz", 0)
    current = mix(current, other, level_weights[3])
    padded = extended(current, (("gx", 0), ("gy", 1), ("gz", 2)), 1)
    neighbours = (
        padded[:-2, 1:-1, 1:-1],
        padded[2:, 1:-1, 1:-1],
        padded[1:-1, :-2, 1:-1],
        padded[1:-1, 2:, 1:-1],
        padded[1:-1, 1:-1, :-2],
        padded[1:-1, 1:-1, 2:],
    )
    total = current.astype(jnp.float32)
    for index in range(6):
        total = total + apply_map(coupling[index], neighbours[index])
    grid = total.astype(jnp.bfloat16)
    leaf_count = grid.shape[0] * grid.shape[1] * grid.shape[2]
    leaf_grid = grid.reshape(leaf_count, grid.shape[3], grid.shape[4])
    return sample(leaf_grid, positions, block_leaf, block_count)


def solution(mesh):
    placed = (
        P("gx", "gy", "gz", None, None),
        P(),
        P(),
        P(None, ("gx", "gy", "gz")),
        P(("gx", "gy", "gz")),
        P(("gx", "gy", "gz")),
    )
    return jax.shard_map(
        local, mesh=mesh, in_specs=placed, out_specs=P(("gx", "gy", "gz"), None), check_vma=False
    )
```

```python
import math

import numpy as np
import jax
import jax.numpy as jnp
from jax import lax
from jax.experimental import pallas as pl
from jax.experimental.pallas import tpu as pltpu
from jax.sharding import PartitionSpec as P

PTS = 8
ROWS = 128
BLOCKS_PER_STEP = 8

NODES = [
    float(v)
    for v in np.cos(
        np.float32(math.pi) * (np.float32(2.0) * np.arange(PTS, dtype=np.float32) + np.float32(1.0)) / np.float32(2.0 * PTS)
    ).astype(np.float32)
]


def from_partner(shard, axis, apart):
    return lax.ppermute(shard, axis, [(i, i ^ 1 << apart) for i in range(lax.axis_size(axis))])


def extended(cells, sides, width):
    for axis, dim in sides:
        count = lax.axis_size(axis)
        ends = count - 1
        head = lax.slice_in_dim(cells, 0, width, axis=dim)
        tail = lax.slice_in_dim(cells, cells.shape[dim] - width, cells.shape[dim], axis=dim)
        cells = jnp.concatenate(
            [
                lax.ppermute(tail, axis, [(i, (i + 1) % count) for i in range(ends)]),
                cells,
                lax.ppermute(head, axis, [((i + 1) % count, i) for i in range(ends)]),
            ],
            axis=dim,
        )
    return cells


def swapped(block):
    half = block.shape[-1] // 2
    return jnp.concatenate([-block[..., half:], block[..., :half]], axis=-1)


def apply_map(weights, block):
    return jnp.einsum("jk,...kc->...jc", weights, block, preferred_element_type=jnp.float32)


def mix(block, other, weights):
    total = apply_map(weights[0, 0], block) + apply_map(weights[0, 1], swapped(block))
    total = total + apply_map(weights[1, 0], other) + apply_map(weights[1, 1], swapped(other))
    return total.astype(jnp.bfloat16)


def basis(u, row):
    ub = jnp.broadcast_to(u, (PTS, ROWS))
    tcol = jnp.zeros((PTS, ROWS), jnp.float32)
    for j in range(PTS):
        tcol = jnp.where(row == j, NODES[j], tcol)
    term = jnp.ones((PTS, ROWS), jnp.float32)
    for m in range(PTS):
        own = row == m
        num = jnp.where(own, 1.0, ub - NODES[m])
        den = jnp.where(own, 1.0, tcol - NODES[m])
        term = term * num / den
    return term


def sample_kernel(leaf_ref, count_ref, pos_ref, grid_ref, out_ref):
    step = pl.program_id(0)
    row = lax.broadcasted_iota(jnp.int32, (PTS, ROWS), 0)
    live_row = lax.broadcasted_iota(jnp.int32, (ROWS, out_ref.shape[1]), 0)
    for i in range(BLOCKS_PER_STEP):
        b = step * BLOCKS_PER_STEP + i
        u = pos_ref[:, i * ROWS:(i + 1) * ROWS]
        lx = basis(u[0:1, :], row)
        ly = basis(u[1:2, :], row)
        lz = basis(u[2:3, :], row)
        pieces = []
        for jx in range(PTS):
            bx = jnp.broadcast_to(lx[jx:jx + 1, :], (PTS, ROWS))
            for jy in range(PTS):
                by = jnp.broadcast_to(ly[jy:jy + 1, :], (PTS, ROWS))
                pieces.append((bx * by) * lz)
        weights_t = jnp.concatenate(pieces, axis=0).astype(jnp.bfloat16)
        leaf = grid_ref[leaf_ref[b]]
        values = lax.dot_general(
            weights_t, leaf, (((0,), (0,)), ((), ())), preferred_element_type=jnp.float32
        )
        values = jnp.where(live_row < count_ref[b], values, 0.0)
        out_ref[i * ROWS:(i + 1) * ROWS, :] = values.astype(out_ref.dtype)


def sample(leaf_grid, positions, block_leaf, block_count):
    leaves, cheb, cols = leaf_grid.shape
    blocks = block_leaf.shape[0]
    width = BLOCKS_PER_STEP * ROWS
    spec = pltpu.PrefetchScalarGridSpec(
        num_scalar_prefetch=2,
        grid=(blocks // BLOCKS_PER_STEP,),
        in_specs=[
            pl.BlockSpec((3, width), lambda s, lf, ct: (0, s)),
            pl.BlockSpec((leaves, cheb, cols), lambda s, lf, ct: (0, 0, 0)),
        ],
        out_specs=pl.BlockSpec((width, cols), lambda s, lf, ct: (s, 0)),
    )
    return pl.pallas_call(
        sample_kernel,
        grid_spec=spec,
        out_shape=jax.ShapeDtypeStruct((blocks * ROWS, cols), jnp.bfloat16),
    )(block_leaf, block_count, positions, leaf_grid)


def butterfly(cells, level_weights):
    for level in range(2):
        cells = mix(cells, from_partner(cells, "gx", level), level_weights[level])
    cells = mix(cells, from_partner(cells, "gy", 0), level_weights[2])
    return mix(cells, from_partner(cells, "gz", 0), level_weights[3])


LEVEL_PLAN = (("gx", 0), ("gx", 1), ("gy", 0), ("gz", 0))


def pipelined(coefficients, level_weights, chunks):
    cells = [coefficients[:, k:k + 1] for k in range(chunks)]
    levels = len(LEVEL_PLAN)
    for tick in range(chunks + levels - 1):
        active = [k for k in range(chunks) if 0 <= tick - k < levels]
        ready = lax.optimization_barrier(tuple(cells[k] for k in active))
        for k, block in zip(active, ready):
            level = tick - k
            axis, bit = LEVEL_PLAN[level]
            cells[k] = mix(block, from_partner(block, axis, bit), level_weights[level])
    return cells


def from_below(slab, axis):
    count = lax.axis_size(axis)
    return lax.ppermute(slab, axis, [(i, i + 1) for i in range(count - 1)])


def from_above(slab, axis):
    count = lax.axis_size(axis)
    return lax.ppermute(slab, axis, [(i + 1, i) for i in range(count - 1)])


def faces(cells, axis, dim):
    size = cells.shape[dim]
    first = lax.slice_in_dim(cells, 0, 1, axis=dim)
    last = lax.slice_in_dim(cells, size - 1, size, axis=dim)
    below = jnp.concatenate([from_below(last, axis), lax.slice_in_dim(cells, 0, size - 1, axis=dim)], axis=dim)
    above = jnp.concatenate([lax.slice_in_dim(cells, 1, size, axis=dim), from_above(first, axis)], axis=dim)
    return below, above


def local(coefficients, level_weights, coupling, positions, block_leaf, block_count):
    chunks = coefficients.shape[1]
    done = pipelined(coefficients, level_weights, chunks)
    low_y = from_below(done[chunks - 1], "gy")
    high_y = from_above(done[0], "gy")
    grids = []
    for k in range(chunks):
        cells = done[k]
        minus_x, plus_x = faces(cells, "gx", 0)
        minus_z, plus_z = faces(cells, "gz", 2)
        minus_y = done[k - 1] if k > 0 else low_y
        plus_y = done[k + 1] if k < chunks - 1 else high_y
        neighbours = (minus_x, plus_x, minus_y, plus_y, minus_z, plus_z)
        total = cells.astype(jnp.float32)
        for index in range(6):
            total = total + apply_map(coupling[index], neighbours[index])
        grids.append(total.astype(jnp.bfloat16))
    grid = jnp.concatenate(grids, axis=1)
    leaf_count = grid.shape[0] * grid.shape[1] * grid.shape[2]
    leaf_grid = grid.reshape(leaf_count, grid.shape[3], grid.shape[4])
    return sample(leaf_grid, positions, block_leaf, block_count)


def solution(mesh):
    placed = (
        P("gx", "gy", "gz", None, None),
        P(),
        P(),
        P(None, ("gx", "gy", "gz")),
        P(("gx", "gy", "gz")),
        P(("gx", "gy", "gz")),
    )
    return jax.shard_map(
        local, mesh=mesh, in_specs=placed, out_specs=P(("gx", "gy", "gz"), None), check_vma=False
    )
```

```python
import math

import numpy as np
import jax
import jax.numpy as jnp
from jax import lax
from jax.experimental import pallas as pl
from jax.experimental.pallas import tpu as pltpu
from jax.sharding import PartitionSpec as P

PTS = 8
ROWS = 128
BLOCKS_PER_STEP = 8

NODES = [
    float(v)
    for v in np.cos(
        np.float32(math.pi) * (np.float32(2.0) * np.arange(PTS, dtype=np.float32) + np.float32(1.0)) / np.float32(2.0 * PTS)
    ).astype(np.float32)
]


def from_partner(shard, axis, apart):
    return lax.ppermute(shard, axis, [(i, i ^ 1 << apart) for i in range(lax.axis_size(axis))])


def extended(cells, sides, width):
    for axis, dim in sides:
        count = lax.axis_size(axis)
        ends = count - 1
        head = lax.slice_in_dim(cells, 0, width, axis=dim)
        tail = lax.slice_in_dim(cells, cells.shape[dim] - width, cells.shape[dim], axis=dim)
        cells = jnp.concatenate(
            [
                lax.ppermute(tail, axis, [(i, (i + 1) % count) for i in range(ends)]),
                cells,
                lax.ppermute(head, axis, [((i + 1) % count, i) for i in range(ends)]),
            ],
            axis=dim,
        )
    return cells


def swapped(block):
    half = block.shape[-1] // 2
    return jnp.concatenate([-block[..., half:], block[..., :half]], axis=-1)


def apply_map(weights, block):
    return jnp.einsum("jk,...kc->...jc", weights, block, preferred_element_type=jnp.float32)


def mix(block, other, weights):
    total = apply_map(weights[0, 0], block) + apply_map(weights[0, 1], swapped(block))
    total = total + apply_map(weights[1, 0], other) + apply_map(weights[1, 1], swapped(other))
    return total.astype(jnp.bfloat16)


def basis(u, row):
    ub = jnp.broadcast_to(u, (PTS, ROWS))
    tcol = jnp.zeros((PTS, ROWS), jnp.float32)
    for j in range(PTS):
        tcol = jnp.where(row == j, NODES[j], tcol)
    term = jnp.ones((PTS, ROWS), jnp.float32)
    for m in range(PTS):
        own = row == m
        num = jnp.where(own, 1.0, ub - NODES[m])
        den = jnp.where(own, 1.0, tcol - NODES[m])
        term = term * num / den
    return term


def sample_kernel(leaf_ref, count_ref, pos_ref, grid_ref, out_ref):
    step = pl.program_id(0)
    row = lax.broadcasted_iota(jnp.int32, (PTS, ROWS), 0)
    live_row = lax.broadcasted_iota(jnp.int32, (ROWS, out_ref.shape[1]), 0)
    for i in range(BLOCKS_PER_STEP):
        b = step * BLOCKS_PER_STEP + i
        u = pos_ref[:, i * ROWS:(i + 1) * ROWS]
        lx = basis(u[0:1, :], row)
        ly = basis(u[1:2, :], row)
        lz = basis(u[2:3, :], row)
        pieces = []
        for jx in range(PTS):
            bx = jnp.broadcast_to(lx[jx:jx + 1, :], (PTS, ROWS))
            for jy in range(PTS):
                by = jnp.broadcast_to(ly[jy:jy + 1, :], (PTS, ROWS))
                pieces.append((bx * by) * lz)
        weights_t = jnp.concatenate(pieces, axis=0).astype(jnp.bfloat16)
        leaf = grid_ref[leaf_ref[b]]
        values = lax.dot_general(
            weights_t, leaf, (((0,), (0,)), ((), ())), preferred_element_type=jnp.float32
        )
        values = jnp.where(live_row < count_ref[b], values, 0.0)
        out_ref[i * ROWS:(i + 1) * ROWS, :] = values.astype(out_ref.dtype)


def sample(leaf_grid, positions, block_leaf, block_count):
    leaves, cheb, cols = leaf_grid.shape
    blocks = block_leaf.shape[0]
    width = BLOCKS_PER_STEP * ROWS
    spec = pltpu.PrefetchScalarGridSpec(
        num_scalar_prefetch=2,
        grid=(blocks // BLOCKS_PER_STEP,),
        in_specs=[
            pl.BlockSpec((3, width), lambda s, lf, ct: (0, s)),
            pl.BlockSpec((leaves, cheb, cols), lambda s, lf, ct: (0, 0, 0)),
        ],
        out_specs=pl.BlockSpec((width, cols), lambda s, lf, ct: (s, 0)),
    )
    return pl.pallas_call(
        sample_kernel,
        grid_spec=spec,
        out_shape=jax.ShapeDtypeStruct((blocks * ROWS, cols), jnp.bfloat16),
    )(block_leaf, block_count, positions, leaf_grid)


def butterfly(cells, level_weights):
    for level in range(2):
        cells = mix(cells, from_partner(cells, "gx", level), level_weights[level])
    cells = mix(cells, from_partner(cells, "gy", 0), level_weights[2])
    return mix(cells, from_partner(cells, "gz", 0), level_weights[3])


LEVEL_PLAN = (("gx", 0), ("gx", 1), ("gy", 0), ("gz", 0))


def pipelined(coefficients, level_weights, chunks):
    cells = [coefficients[:, k:k + 1] for k in range(chunks)]
    levels = len(LEVEL_PLAN)
    for tick in range(chunks + levels - 1):
        active = [k for k in range(chunks) if 0 <= tick - k < levels]
        ready = lax.optimization_barrier(tuple(cells[k] for k in active))
        for k, block in zip(active, ready):
            level = tick - k
            axis, bit = LEVEL_PLAN[level]
            cells[k] = mix(block, from_partner(block, axis, bit), level_weights[level])
    return cells


def from_below(slab, axis):
    count = lax.axis_size(axis)
    return lax.ppermute(slab, axis, [(i, i + 1) for i in range(count - 1)])


def from_above(slab, axis):
    count = lax.axis_size(axis)
    return lax.ppermute(slab, axis, [(i + 1, i) for i in range(count - 1)])


def faces(cells, axis, dim):
    size = cells.shape[dim]
    first = lax.slice_in_dim(cells, 0, 1, axis=dim)
    last = lax.slice_in_dim(cells, size - 1, size, axis=dim)
    below = jnp.concatenate([from_below(last, axis), lax.slice_in_dim(cells, 0, size - 1, axis=dim)], axis=dim)
    above = jnp.concatenate([lax.slice_in_dim(cells, 1, size, axis=dim), from_above(first, axis)], axis=dim)
    return below, above


def local(coefficients, level_weights, coupling, positions, block_leaf, block_count):
    chunks = coefficients.shape[1]
    cells = jnp.concatenate(pipelined(coefficients, level_weights, chunks), axis=1)
    minus_x, plus_x = faces(cells, "gx", 0)
    minus_y, plus_y = faces(cells, "gy", 1)
    minus_z, plus_z = faces(cells, "gz", 2)
    neighbours = (minus_x, plus_x, minus_y, plus_y, minus_z, plus_z)
    total = cells.astype(jnp.float32)
    for index in range(6):
        total = total + apply_map(coupling[index], neighbours[index])
    grid = total.astype(jnp.bfloat16)
    leaf_count = grid.shape[0] * grid.shape[1] * grid.shape[2]
    leaf_grid = grid.reshape(leaf_count, grid.shape[3], grid.shape[4])
    return sample(leaf_grid, positions, block_leaf, block_count)


def solution(mesh):
    placed = (
        P("gx", "gy", "gz", None, None),
        P(),
        P(),
        P(None, ("gx", "gy", "gz")),
        P(("gx", "gy", "gz")),
        P(("gx", "gy", "gz")),
    )
    return jax.shard_map(
        local, mesh=mesh, in_specs=placed, out_specs=P(("gx", "gy", "gz"), None), check_vma=False
    )
```

```python
import math

import numpy as np
import jax
import jax.numpy as jnp
from jax import lax
from jax.experimental import pallas as pl
from jax.experimental.pallas import tpu as pltpu
from jax.sharding import PartitionSpec as P

PTS = 8
ROWS = 128
BLOCKS_PER_STEP = 8

NODES = [
    float(v)
    for v in np.cos(
        np.float32(math.pi) * (np.float32(2.0) * np.arange(PTS, dtype=np.float32) + np.float32(1.0)) / np.float32(2.0 * PTS)
    ).astype(np.float32)
]


def from_partner(shard, axis, apart):
    return lax.ppermute(shard, axis, [(i, i ^ 1 << apart) for i in range(lax.axis_size(axis))])


def extended(cells, sides, width):
    for axis, dim in sides:
        count = lax.axis_size(axis)
        ends = count - 1
        head = lax.slice_in_dim(cells, 0, width, axis=dim)
        tail = lax.slice_in_dim(cells, cells.shape[dim] - width, cells.shape[dim], axis=dim)
        cells = jnp.concatenate(
            [
                lax.ppermute(tail, axis, [(i, (i + 1) % count) for i in range(ends)]),
                cells,
                lax.ppermute(head, axis, [((i + 1) % count, i) for i in range(ends)]),
            ],
            axis=dim,
        )
    return cells


def swapped(block):
    half = block.shape[-1] // 2
    return jnp.concatenate([-block[..., half:], block[..., :half]], axis=-1)


def apply_map(weights, block):
    return jnp.einsum("jk,...kc->...jc", weights, block, preferred_element_type=jnp.float32)


def mix(block, other, weights):
    total = apply_map(weights[0, 0], block) + apply_map(weights[0, 1], swapped(block))
    total = total + apply_map(weights[1, 0], other) + apply_map(weights[1, 1], swapped(other))
    return total.astype(jnp.bfloat16)


def basis(u, row):
    ub = jnp.broadcast_to(u, (PTS, ROWS))
    tcol = jnp.zeros((PTS, ROWS), jnp.float32)
    for j in range(PTS):
        tcol = jnp.where(row == j, NODES[j], tcol)
    term = jnp.ones((PTS, ROWS), jnp.float32)
    for m in range(PTS):
        own = row == m
        num = jnp.where(own, 1.0, ub - NODES[m])
        den = jnp.where(own, 1.0, tcol - NODES[m])
        term = term * num / den
    return term


def sample_kernel(leaf_ref, count_ref, pos_ref, grid_ref, out_ref):
    step = pl.program_id(0)
    row = lax.broadcasted_iota(jnp.int32, (PTS, ROWS), 0)
    live_row = lax.broadcasted_iota(jnp.int32, (ROWS, out_ref.shape[1]), 0)
    for i in range(BLOCKS_PER_STEP):
        b = step * BLOCKS_PER_STEP + i
        u = pos_ref[:, i * ROWS:(i + 1) * ROWS]
        lx = basis(u[0:1, :], row)
        ly = basis(u[1:2, :], row)
        lz = basis(u[2:3, :], row)
        pieces = []
        for jx in range(PTS):
            bx = jnp.broadcast_to(lx[jx:jx + 1, :], (PTS, ROWS))
            for jy in range(PTS):
                by = jnp.broadcast_to(ly[jy:jy + 1, :], (PTS, ROWS))
                pieces.append((bx * by) * lz)
        weights_t = jnp.concatenate(pieces, axis=0).astype(jnp.bfloat16)
        leaf = grid_ref[leaf_ref[b]]
        values = lax.dot_general(
            weights_t, leaf, (((0,), (0,)), ((), ())), preferred_element_type=jnp.float32
        )
        values = jnp.where(live_row < count_ref[b], values, 0.0)
        out_ref[i * ROWS:(i + 1) * ROWS, :] = values.astype(out_ref.dtype)


def sample(leaf_grid, positions, block_leaf, block_count):
    leaves, cheb, cols = leaf_grid.shape
    blocks = block_leaf.shape[0]
    width = BLOCKS_PER_STEP * ROWS
    spec = pltpu.PrefetchScalarGridSpec(
        num_scalar_prefetch=2,
        grid=(blocks // BLOCKS_PER_STEP,),
        in_specs=[
            pl.BlockSpec((3, width), lambda s, lf, ct: (0, s)),
            pl.BlockSpec((leaves, cheb, cols), lambda s, lf, ct: (0, 0, 0)),
        ],
        out_specs=pl.BlockSpec((width, cols), lambda s, lf, ct: (s, 0)),
    )
    return pl.pallas_call(
        sample_kernel,
        grid_spec=spec,
        out_shape=jax.ShapeDtypeStruct((blocks * ROWS, cols), jnp.bfloat16),
    )(block_leaf, block_count, positions, leaf_grid)


def butterfly(cells, level_weights):
    for level in range(2):
        cells = mix(cells, from_partner(cells, "gx", level), level_weights[level])
    cells = mix(cells, from_partner(cells, "gy", 0), level_weights[2])
    return mix(cells, from_partner(cells, "gz", 0), level_weights[3])


LEVEL_PLAN = (("gx", 0), ("gx", 1), ("gy", 0), ("gz", 0))


def pipelined(coefficients, level_weights, chunks):
    cells = [coefficients[:, k:k + 1] for k in range(chunks)]
    partner_faces = [None] * chunks
    levels = len(LEVEL_PLAN)
    side = lax.axis_index("gz") % 2
    for tick in range(chunks + levels - 1):
        active = [k for k in range(chunks) if 0 <= tick - k < levels]
        ready = lax.optimization_barrier(tuple(cells[k] for k in active))
        for k, block in zip(active, ready):
            level = tick - k
            axis, bit = LEVEL_PLAN[level]
            other = from_partner(block, axis, bit)
            cells[k] = mix(block, other, level_weights[level])
            if level == levels - 1:
                partner_faces[k] = mix(
                    lax.dynamic_slice_in_dim(other, side, 1, axis=2),
                    lax.dynamic_slice_in_dim(block, side, 1, axis=2),
                    level_weights[level],
                )
    return cells, partner_faces


def z_faces(cells, partner_face):
    count = lax.axis_size("gz")
    side = lax.axis_index("gz") % 2
    pairs = [(i, i - 1) for i in range(2, count, 2)] + [(i, i + 1) for i in range(1, count - 1, 2)]
    sent = lax.ppermute(lax.dynamic_slice_in_dim(cells, side, 1, axis=2), "gz", pairs)
    even = side == 0
    below = jnp.where(even, sent, partner_face)
    above = jnp.where(even, partner_face, sent)
    size = cells.shape[2]
    minus = jnp.concatenate([below, lax.slice_in_dim(cells, 0, size - 1, axis=2)], axis=2)
    plus = jnp.concatenate([lax.slice_in_dim(cells, 1, size, axis=2), above], axis=2)
    return minus, plus


def from_below(slab, axis):
    count = lax.axis_size(axis)
    return lax.ppermute(slab, axis, [(i, i + 1) for i in range(count - 1)])


def from_above(slab, axis):
    count = lax.axis_size(axis)
    return lax.ppermute(slab, axis, [(i + 1, i) for i in range(count - 1)])


def faces(cells, axis, dim):
    size = cells.shape[dim]
    first = lax.slice_in_dim(cells, 0, 1, axis=dim)
    last = lax.slice_in_dim(cells, size - 1, size, axis=dim)
    below = jnp.concatenate([from_below(last, axis), lax.slice_in_dim(cells, 0, size - 1, axis=dim)], axis=dim)
    above = jnp.concatenate([lax.slice_in_dim(cells, 1, size, axis=dim), from_above(first, axis)], axis=dim)
    return below, above


def local(coefficients, level_weights, coupling, positions, block_leaf, block_count):
    chunks = coefficients.shape[1]
    done, partner_faces = pipelined(coefficients, level_weights, chunks)
    cells = jnp.concatenate(done, axis=1)
    partner_face = jnp.concatenate(partner_faces, axis=1)
    minus_x, plus_x = faces(cells, "gx", 0)
    minus_y, plus_y = faces(cells, "gy", 1)
    minus_z, plus_z = z_faces(cells, partner_face)
    neighbours = (minus_x, plus_x, minus_y, plus_y, minus_z, plus_z)
    total = cells.astype(jnp.float32)
    for index in range(6):
        total = total + apply_map(coupling[index], neighbours[index])
    grid = total.astype(jnp.bfloat16)
    leaf_count = grid.shape[0] * grid.shape[1] * grid.shape[2]
    leaf_grid = grid.reshape(leaf_count, grid.shape[3], grid.shape[4])
    return sample(leaf_grid, positions, block_leaf, block_count)


def solution(mesh):
    placed = (
        P("gx", "gy", "gz", None, None),
        P(),
        P(),
        P(None, ("gx", "gy", "gz")),
        P(("gx", "gy", "gz")),
        P(("gx", "gy", "gz")),
    )
    return jax.shard_map(
        local, mesh=mesh, in_specs=placed, out_specs=P(("gx", "gy", "gz"), None), check_vma=False
    )
```

```python
import math

import numpy as np
import jax
import jax.numpy as jnp
from jax import lax
from jax.experimental import pallas as pl
from jax.experimental.pallas import tpu as pltpu
from jax.sharding import PartitionSpec as P

PTS = 8
ROWS = 128
BLOCKS_PER_STEP = 8

NODES = [
    float(v)
    for v in np.cos(
        np.float32(math.pi) * (np.float32(2.0) * np.arange(PTS, dtype=np.float32) + np.float32(1.0)) / np.float32(2.0 * PTS)
    ).astype(np.float32)
]


def from_partner(shard, axis, apart):
    return lax.ppermute(shard, axis, [(i, i ^ 1 << apart) for i in range(lax.axis_size(axis))])


def extended(cells, sides, width):
    for axis, dim in sides:
        count = lax.axis_size(axis)
        ends = count - 1
        head = lax.slice_in_dim(cells, 0, width, axis=dim)
        tail = lax.slice_in_dim(cells, cells.shape[dim] - width, cells.shape[dim], axis=dim)
        cells = jnp.concatenate(
            [
                lax.ppermute(tail, axis, [(i, (i + 1) % count) for i in range(ends)]),
                cells,
                lax.ppermute(head, axis, [((i + 1) % count, i) for i in range(ends)]),
            ],
            axis=dim,
        )
    return cells


def swapped(block):
    half = block.shape[-1] // 2
    return jnp.concatenate([-block[..., half:], block[..., :half]], axis=-1)


def apply_map(weights, block):
    return jnp.einsum("jk,...kc->...jc", weights, block, preferred_element_type=jnp.float32)


def mix(block, other, weights):
    total = apply_map(weights[0, 0], block) + apply_map(weights[0, 1], swapped(block))
    total = total + apply_map(weights[1, 0], other) + apply_map(weights[1, 1], swapped(other))
    return total.astype(jnp.bfloat16)


def basis(u, row):
    ub = jnp.broadcast_to(u, (PTS, ROWS))
    tcol = jnp.zeros((PTS, ROWS), jnp.float32)
    for j in range(PTS):
        tcol = jnp.where(row == j, NODES[j], tcol)
    term = jnp.ones((PTS, ROWS), jnp.float32)
    for m in range(PTS):
        own = row == m
        num = jnp.where(own, 1.0, ub - NODES[m])
        den = jnp.where(own, 1.0, tcol - NODES[m])
        term = term * num / den
    return term


def sample_kernel(leaf_ref, count_ref, pos_ref, grid_ref, out_ref):
    step = pl.program_id(0)
    row = lax.broadcasted_iota(jnp.int32, (PTS, ROWS), 0)
    live_row = lax.broadcasted_iota(jnp.int32, (ROWS, out_ref.shape[1]), 0)
    for i in range(BLOCKS_PER_STEP):
        b = step * BLOCKS_PER_STEP + i
        u = pos_ref[:, i * ROWS:(i + 1) * ROWS]
        lx = basis(u[0:1, :], row)
        ly = basis(u[1:2, :], row)
        lz = basis(u[2:3, :], row)
        pieces = []
        for jx in range(PTS):
            bx = jnp.broadcast_to(lx[jx:jx + 1, :], (PTS, ROWS))
            for jy in range(PTS):
                by = jnp.broadcast_to(ly[jy:jy + 1, :], (PTS, ROWS))
                pieces.append((bx * by) * lz)
        weights_t = jnp.concatenate(pieces, axis=0).astype(jnp.bfloat16)
        leaf = grid_ref[leaf_ref[b]]
        values = lax.dot_general(
            weights_t, leaf, (((0,), (0,)), ((), ())), preferred_element_type=jnp.float32
        )
        values = jnp.where(live_row < count_ref[b], values, 0.0)
        out_ref[i * ROWS:(i + 1) * ROWS, :] = values.astype(out_ref.dtype)


def sample(leaf_grid, positions, block_leaf, block_count):
    leaves, cheb, cols = leaf_grid.shape
    blocks = block_leaf.shape[0]
    width = BLOCKS_PER_STEP * ROWS
    spec = pltpu.PrefetchScalarGridSpec(
        num_scalar_prefetch=2,
        grid=(blocks // BLOCKS_PER_STEP,),
        in_specs=[
            pl.BlockSpec((3, width), lambda s, lf, ct: (0, s)),
            pl.BlockSpec((leaves, cheb, cols), lambda s, lf, ct: (0, 0, 0)),
        ],
        out_specs=pl.BlockSpec((width, cols), lambda s, lf, ct: (s, 0)),
    )
    return pl.pallas_call(
        sample_kernel,
        grid_spec=spec,
        out_shape=jax.ShapeDtypeStruct((blocks * ROWS, cols), jnp.bfloat16),
    )(block_leaf, block_count, positions, leaf_grid)


def butterfly(cells, level_weights):
    for level in range(2):
        cells = mix(cells, from_partner(cells, "gx", level), level_weights[level])
    cells = mix(cells, from_partner(cells, "gy", 0), level_weights[2])
    return mix(cells, from_partner(cells, "gz", 0), level_weights[3])


LEVEL_PLAN = (("gx", 0), ("gx", 1), ("gy", 0), ("gz", 0))


def pipelined(coefficients, level_weights, chunks):
    cells = [coefficients[:, k:k + 1] for k in range(chunks)]
    partner_faces = [None] * chunks
    levels = len(LEVEL_PLAN)
    side = lax.axis_index("gz") % 2
    for tick in range(chunks + levels - 1):
        active = [k for k in range(chunks) if 0 <= tick - k < levels]
        ready = lax.optimization_barrier(tuple(cells[k] for k in active))
        for k, block in zip(active, ready):
            level = tick - k
            axis, bit = LEVEL_PLAN[level]
            other = from_partner(block, axis, bit)
            cells[k] = mix(block, other, level_weights[level])
            if level == levels - 1:
                partner_faces[k] = (
                    lax.dynamic_slice_in_dim(other, side, 1, axis=2),
                    lax.dynamic_slice_in_dim(block, side, 1, axis=2),
                )
    return cells, partner_faces


def z_faces(cells, partner_face):
    count = lax.axis_size("gz")
    side = lax.axis_index("gz") % 2
    pairs = [(i, i - 1) for i in range(2, count, 2)] + [(i, i + 1) for i in range(1, count - 1, 2)]
    sent = lax.ppermute(lax.dynamic_slice_in_dim(cells, side, 1, axis=2), "gz", pairs)
    even = side == 0
    below = jnp.where(even, sent, partner_face)
    above = jnp.where(even, partner_face, sent)
    size = cells.shape[2]
    minus = jnp.concatenate([below, lax.slice_in_dim(cells, 0, size - 1, axis=2)], axis=2)
    plus = jnp.concatenate([lax.slice_in_dim(cells, 1, size, axis=2), above], axis=2)
    return minus, plus


def from_below(slab, axis):
    count = lax.axis_size(axis)
    return lax.ppermute(slab, axis, [(i, i + 1) for i in range(count - 1)])


def from_above(slab, axis):
    count = lax.axis_size(axis)
    return lax.ppermute(slab, axis, [(i + 1, i) for i in range(count - 1)])


def faces(cells, axis, dim):
    size = cells.shape[dim]
    first = lax.slice_in_dim(cells, 0, 1, axis=dim)
    last = lax.slice_in_dim(cells, size - 1, size, axis=dim)
    below = jnp.concatenate([from_below(last, axis), lax.slice_in_dim(cells, 0, size - 1, axis=dim)], axis=dim)
    above = jnp.concatenate([lax.slice_in_dim(cells, 1, size, axis=dim), from_above(first, axis)], axis=dim)
    return below, above


def local(coefficients, level_weights, coupling, positions, block_leaf, block_count):
    chunks = coefficients.shape[1]
    done, partner_slabs = pipelined(coefficients, level_weights, chunks)
    done[-1], partner_slabs = lax.optimization_barrier((done[-1], partner_slabs))
    cells = jnp.concatenate(done, axis=1)
    partner_face = mix(
        jnp.concatenate([theirs for theirs, _ in partner_slabs], axis=1),
        jnp.concatenate([ours for _, ours in partner_slabs], axis=1),
        level_weights[len(LEVEL_PLAN) - 1],
    )
    minus_x, plus_x = faces(cells, "gx", 0)
    minus_y, plus_y = faces(cells, "gy", 1)
    minus_z, plus_z = z_faces(cells, partner_face)
    neighbours = (minus_x, plus_x, minus_y, plus_y, minus_z, plus_z)
    total = cells.astype(jnp.float32)
    for index in range(6):
        total = total + apply_map(coupling[index], neighbours[index])
    grid = total.astype(jnp.bfloat16)
    leaf_count = grid.shape[0] * grid.shape[1] * grid.shape[2]
    leaf_grid = grid.reshape(leaf_count, grid.shape[3], grid.shape[4])
    return sample(leaf_grid, positions, block_leaf, block_count)


def solution(mesh):
    placed = (
        P("gx", "gy", "gz", None, None),
        P(),
        P(),
        P(None, ("gx", "gy", "gz")),
        P(("gx", "gy", "gz")),
        P(("gx", "gy", "gz")),
    )
    return jax.shard_map(
        local, mesh=mesh, in_specs=placed, out_specs=P(("gx", "gy", "gz"), None), check_vma=False
    )
```

```python
import math

import numpy as np
import jax
import jax.numpy as jnp
from jax import lax
from jax.experimental import pallas as pl
from jax.experimental.pallas import tpu as pltpu
from jax.sharding import PartitionSpec as P

PTS = 8
ROWS = 128
BLOCKS_PER_STEP = 8

NODES = [
    float(v)
    for v in np.cos(
        np.float32(math.pi) * (np.float32(2.0) * np.arange(PTS, dtype=np.float32) + np.float32(1.0)) / np.float32(2.0 * PTS)
    ).astype(np.float32)
]


def from_partner(shard, axis, apart):
    return lax.ppermute(shard, axis, [(i, i ^ 1 << apart) for i in range(lax.axis_size(axis))])


def extended(cells, sides, width):
    for axis, dim in sides:
        count = lax.axis_size(axis)
        ends = count - 1
        head = lax.slice_in_dim(cells, 0, width, axis=dim)
        tail = lax.slice_in_dim(cells, cells.shape[dim] - width, cells.shape[dim], axis=dim)
        cells = jnp.concatenate(
            [
                lax.ppermute(tail, axis, [(i, (i + 1) % count) for i in range(ends)]),
                cells,
                lax.ppermute(head, axis, [((i + 1) % count, i) for i in range(ends)]),
            ],
            axis=dim,
        )
    return cells


def swapped(block):
    half = block.shape[-1] // 2
    return jnp.concatenate([-block[..., half:], block[..., :half]], axis=-1)


def apply_map(weights, block):
    return jnp.einsum("jk,...kc->...jc", weights, block, preferred_element_type=jnp.float32)


def mix(block, other, weights):
    total = apply_map(weights[0, 0], block) + apply_map(weights[0, 1], swapped(block))
    total = total + apply_map(weights[1, 0], other) + apply_map(weights[1, 1], swapped(other))
    return total.astype(jnp.bfloat16)


def basis(u, row):
    ub = jnp.broadcast_to(u, (PTS, ROWS))
    tcol = jnp.zeros((PTS, ROWS), jnp.float32)
    for j in range(PTS):
        tcol = jnp.where(row == j, NODES[j], tcol)
    term = jnp.ones((PTS, ROWS), jnp.float32)
    for m in range(PTS):
        own = row == m
        num = jnp.where(own, 1.0, ub - NODES[m])
        den = jnp.where(own, 1.0, tcol - NODES[m])
        term = term * num / den
    return term


def sample_kernel(leaf_ref, count_ref, pos_ref, grid_ref, out_ref):
    step = pl.program_id(0)
    row = lax.broadcasted_iota(jnp.int32, (PTS, ROWS), 0)
    live_row = lax.broadcasted_iota(jnp.int32, (ROWS, out_ref.shape[1]), 0)
    for i in range(BLOCKS_PER_STEP):
        b = step * BLOCKS_PER_STEP + i
        u = pos_ref[:, i * ROWS:(i + 1) * ROWS]
        lx = basis(u[0:1, :], row)
        ly = basis(u[1:2, :], row)
        lz = basis(u[2:3, :], row)
        pieces = []
        for jx in range(PTS):
            bx = jnp.broadcast_to(lx[jx:jx + 1, :], (PTS, ROWS))
            for jy in range(PTS):
                by = jnp.broadcast_to(ly[jy:jy + 1, :], (PTS, ROWS))
                pieces.append((bx * by) * lz)
        weights_t = jnp.concatenate(pieces, axis=0).astype(jnp.bfloat16)
        leaf = grid_ref[leaf_ref[b]]
        values = lax.dot_general(
            weights_t, leaf, (((0,), (0,)), ((), ())), preferred_element_type=jnp.float32
        )
        values = jnp.where(live_row < count_ref[b], values, 0.0)
        out_ref[i * ROWS:(i + 1) * ROWS, :] = values.astype(out_ref.dtype)


def sample(leaf_grid, positions, block_leaf, block_count):
    leaves, cheb, cols = leaf_grid.shape
    blocks = block_leaf.shape[0]
    width = BLOCKS_PER_STEP * ROWS
    spec = pltpu.PrefetchScalarGridSpec(
        num_scalar_prefetch=2,
        grid=(blocks // BLOCKS_PER_STEP,),
        in_specs=[
            pl.BlockSpec((3, width), lambda s, lf, ct: (0, s)),
            pl.BlockSpec((leaves, cheb, cols), lambda s, lf, ct: (0, 0, 0)),
        ],
        out_specs=pl.BlockSpec((width, cols), lambda s, lf, ct: (s, 0)),
    )
    return pl.pallas_call(
        sample_kernel,
        grid_spec=spec,
        out_shape=jax.ShapeDtypeStruct((blocks * ROWS, cols), jnp.bfloat16),
    )(block_leaf, block_count, positions, leaf_grid)


def butterfly(cells, level_weights):
    for level in range(2):
        cells = mix(cells, from_partner(cells, "gx", level), level_weights[level])
    cells = mix(cells, from_partner(cells, "gy", 0), level_weights[2])
    return mix(cells, from_partner(cells, "gz", 0), level_weights[3])


LEVEL_PLAN = (("gx", 0), ("gx", 1), ("gy", 0), ("gz", 0))


def pipelined(coefficients, level_weights, chunks):
    cells = [coefficients[:, k:k + 1] for k in range(chunks)]
    partner_faces = [None] * chunks
    levels = len(LEVEL_PLAN)
    side = lax.axis_index("gz") % 2
    for tick in range(chunks + levels - 1):
        active = [k for k in range(chunks) if 0 <= tick - k < levels]
        ready = {}
        for k in active:
            if k > 0 and tick - k + 1 < levels:
                ready[k], _ = lax.optimization_barrier((cells[k], cells[k - 1]))
            else:
                ready[k] = cells[k]
        for k in active:
            level = tick - k
            axis, bit = LEVEL_PLAN[level]
            block = ready[k]
            other = from_partner(block, axis, bit)
            cells[k] = mix(block, other, level_weights[level])
            if level == levels - 1:
                partner_faces[k] = (
                    lax.dynamic_slice_in_dim(other, side, 1, axis=2),
                    lax.dynamic_slice_in_dim(block, side, 1, axis=2),
                )
    return cells, partner_faces


def z_faces(cells, partner_face):
    count = lax.axis_size("gz")
    side = lax.axis_index("gz") % 2
    pairs = [(i, i - 1) for i in range(2, count, 2)] + [(i, i + 1) for i in range(1, count - 1, 2)]
    sent = lax.ppermute(lax.dynamic_slice_in_dim(cells, side, 1, axis=2), "gz", pairs)
    even = side == 0
    below = jnp.where(even, sent, partner_face)
    above = jnp.where(even, partner_face, sent)
    size = cells.shape[2]
    minus = jnp.concatenate([below, lax.slice_in_dim(cells, 0, size - 1, axis=2)], axis=2)
    plus = jnp.concatenate([lax.slice_in_dim(cells, 1, size, axis=2), above], axis=2)
    return minus, plus


def from_below(slab, axis):
    count = lax.axis_size(axis)
    return lax.ppermute(slab, axis, [(i, i + 1) for i in range(count - 1)])


def from_above(slab, axis):
    count = lax.axis_size(axis)
    return lax.ppermute(slab, axis, [(i + 1, i) for i in range(count - 1)])


def faces(cells, axis, dim):
    size = cells.shape[dim]
    first = lax.slice_in_dim(cells, 0, 1, axis=dim)
    last = lax.slice_in_dim(cells, size - 1, size, axis=dim)
    below = jnp.concatenate([from_below(last, axis), lax.slice_in_dim(cells, 0, size - 1, axis=dim)], axis=dim)
    above = jnp.concatenate([lax.slice_in_dim(cells, 1, size, axis=dim), from_above(first, axis)], axis=dim)
    return below, above


def local(coefficients, level_weights, coupling, positions, block_leaf, block_count):
    chunks = coefficients.shape[1]
    done, partner_slabs = pipelined(coefficients, level_weights, chunks)
    done[-1], partner_slabs = lax.optimization_barrier((done[-1], partner_slabs))
    cells = jnp.concatenate(done, axis=1)
    partner_face = mix(
        jnp.concatenate([theirs for theirs, _ in partner_slabs], axis=1),
        jnp.concatenate([ours for _, ours in partner_slabs], axis=1),
        level_weights[len(LEVEL_PLAN) - 1],
    )
    minus_x, plus_x = faces(cells, "gx", 0)
    minus_y, plus_y = faces(cells, "gy", 1)
    minus_z, plus_z = z_faces(cells, partner_face)
    neighbours = (minus_x, plus_x, minus_y, plus_y, minus_z, plus_z)
    total = cells.astype(jnp.float32)
    for index in range(6):
        total = total + apply_map(coupling[index], neighbours[index])
    grid = total.astype(jnp.bfloat16)
    leaf_count = grid.shape[0] * grid.shape[1] * grid.shape[2]
    leaf_grid = grid.reshape(leaf_count, grid.shape[3], grid.shape[4])
    return sample(leaf_grid, positions, block_leaf, block_count)


def solution(mesh):
    placed = (
        P("gx", "gy", "gz", None, None),
        P(),
        P(),
        P(None, ("gx", "gy", "gz")),
        P(("gx", "gy", "gz")),
        P(("gx", "gy", "gz")),
    )
    return jax.shard_map(
        local, mesh=mesh, in_specs=placed, out_specs=P(("gx", "gy", "gz"), None), check_vma=False
    )
```

```python
import math

import numpy as np
import jax
import jax.numpy as jnp
from jax import lax
from jax.experimental import pallas as pl
from jax.experimental.pallas import tpu as pltpu
from jax.sharding import PartitionSpec as P

PTS = 8
ROWS = 128
BLOCKS_PER_STEP = 8

NODES = [
    float(v)
    for v in np.cos(
        np.float32(math.pi) * (np.float32(2.0) * np.arange(PTS, dtype=np.float32) + np.float32(1.0)) / np.float32(2.0 * PTS)
    ).astype(np.float32)
]


def from_partner(shard, axis, apart):
    return lax.ppermute(shard, axis, [(i, i ^ 1 << apart) for i in range(lax.axis_size(axis))])


def extended(cells, sides, width):
    for axis, dim in sides:
        count = lax.axis_size(axis)
        ends = count - 1
        head = lax.slice_in_dim(cells, 0, width, axis=dim)
        tail = lax.slice_in_dim(cells, cells.shape[dim] - width, cells.shape[dim], axis=dim)
        cells = jnp.concatenate(
            [
                lax.ppermute(tail, axis, [(i, (i + 1) % count) for i in range(ends)]),
                cells,
                lax.ppermute(head, axis, [((i + 1) % count, i) for i in range(ends)]),
            ],
            axis=dim,
        )
    return cells


def swapped(block):
    half = block.shape[-1] // 2
    return jnp.concatenate([-block[..., half:], block[..., :half]], axis=-1)


def apply_map(weights, block):
    return jnp.einsum("jk,...kc->...jc", weights, block, preferred_element_type=jnp.float32)


def mix(block, other, weights):
    total = apply_map(weights[0, 0], block) + apply_map(weights[0, 1], swapped(block))
    total = total + apply_map(weights[1, 0], other) + apply_map(weights[1, 1], swapped(other))
    return total.astype(jnp.bfloat16)


def basis(u, row):
    ub = jnp.broadcast_to(u, (PTS, ROWS))
    tcol = jnp.zeros((PTS, ROWS), jnp.float32)
    for j in range(PTS):
        tcol = jnp.where(row == j, NODES[j], tcol)
    term = jnp.ones((PTS, ROWS), jnp.float32)
    for m in range(PTS):
        own = row == m
        num = jnp.where(own, 1.0, ub - NODES[m])
        den = jnp.where(own, 1.0, tcol - NODES[m])
        term = term * num / den
    return term


def weight_kernel(pos_ref, out_ref):
    row = lax.broadcasted_iota(jnp.int32, (PTS, ROWS), 0)
    for i in range(BLOCKS_PER_STEP):
        u = pos_ref[:, i * ROWS:(i + 1) * ROWS]
        lx = basis(u[0:1, :], row)
        ly = basis(u[1:2, :], row)
        lz = basis(u[2:3, :], row)
        pieces = []
        for jx in range(PTS):
            bx = jnp.broadcast_to(lx[jx:jx + 1, :], (PTS, ROWS))
            for jy in range(PTS):
                by = jnp.broadcast_to(ly[jy:jy + 1, :], (PTS, ROWS))
                pieces.append((bx * by) * lz)
        out_ref[i] = jnp.concatenate(pieces, axis=0).astype(out_ref.dtype)


def sample_weights(positions):
    blocks = positions.shape[1] // ROWS
    width = BLOCKS_PER_STEP * ROWS
    return pl.pallas_call(
        weight_kernel,
        grid=(blocks // BLOCKS_PER_STEP,),
        in_specs=[pl.BlockSpec((3, width), lambda s: (0, s))],
        out_specs=pl.BlockSpec((BLOCKS_PER_STEP, PTS**3, ROWS), lambda s: (s, 0, 0)),
        out_shape=jax.ShapeDtypeStruct((blocks, PTS**3, ROWS), jnp.bfloat16),
    )(positions)


def sample_kernel(leaf_ref, count_ref, weight_ref, grid_ref, out_ref):
    step = pl.program_id(0)
    live_row = lax.broadcasted_iota(jnp.int32, (ROWS, out_ref.shape[1]), 0)
    for i in range(BLOCKS_PER_STEP):
        b = step * BLOCKS_PER_STEP + i
        leaf = leaf_ref[b]
        place = ((leaf // 2) % 4) * 4 + (leaf // 8) * 2 + leaf % 2
        values = jnp.dot(grid_ref[place], weight_ref[i], preferred_element_type=jnp.float32).T
        values = jnp.where(live_row < count_ref[b], values, 0.0)
        out_ref[i * ROWS:(i + 1) * ROWS, :] = values.astype(out_ref.dtype)


def sample(grid, weights, block_leaf, block_count):
    lx, ly, lz, cheb, cols = grid.shape
    leaf_grid = jnp.transpose(grid, (1, 0, 2, 4, 3)).reshape(ly * lx * lz, cols, cheb)
    blocks = block_leaf.shape[0]
    width = BLOCKS_PER_STEP * ROWS
    spec = pltpu.PrefetchScalarGridSpec(
        num_scalar_prefetch=2,
        grid=(blocks // BLOCKS_PER_STEP,),
        in_specs=[
            pl.BlockSpec((BLOCKS_PER_STEP, cheb, ROWS), lambda s, lf, ct: (s, 0, 0)),
            pl.BlockSpec((lx * ly * lz, cols, cheb), lambda s, lf, ct: (0, 0, 0)),
        ],
        out_specs=pl.BlockSpec((width, cols), lambda s, lf, ct: (s, 0)),
    )
    return pl.pallas_call(
        sample_kernel,
        grid_spec=spec,
        out_shape=jax.ShapeDtypeStruct((blocks * ROWS, cols), jnp.bfloat16),
    )(block_leaf, block_count, weights, leaf_grid)


def butterfly(cells, level_weights):
    for level in range(2):
        cells = mix(cells, from_partner(cells, "gx", level), level_weights[level])
    cells = mix(cells, from_partner(cells, "gy", 0), level_weights[2])
    return mix(cells, from_partner(cells, "gz", 0), level_weights[3])


LEVEL_PLAN = (("gx", 0), ("gx", 1), ("gy", 0), ("gz", 0))
WEIGHTS_TICK = 2


def pipelined(coefficients, level_weights, chunks, positions):
    cells = [coefficients[:, k:k + 1] for k in range(chunks)]
    partner_faces = [None] * chunks
    levels = len(LEVEL_PLAN)
    side = lax.axis_index("gz") % 2
    for tick in range(chunks + levels - 1):
        active = [k for k in range(chunks) if 0 <= tick - k < levels]
        ready = {}
        for k in active:
            if k > 0 and tick - k + 1 < levels:
                ready[k], _ = lax.optimization_barrier((cells[k], cells[k - 1]))
            else:
                ready[k] = cells[k]
        if tick == WEIGHTS_TICK:
            positions, _ = lax.optimization_barrier((positions, ready[active[-1]]))
            weights = sample_weights(positions)
        for k in active:
            level = tick - k
            axis, bit = LEVEL_PLAN[level]
            block = ready[k]
            other = from_partner(block, axis, bit)
            cells[k] = mix(block, other, level_weights[level])
            if level == levels - 1:
                partner_faces[k] = (
                    lax.dynamic_slice_in_dim(other, side, 1, axis=2),
                    lax.dynamic_slice_in_dim(block, side, 1, axis=2),
                )
    return cells, partner_faces, weights


def z_faces(cells, partner_face):
    count = lax.axis_size("gz")
    side = lax.axis_index("gz") % 2
    pairs = [(i, i - 1) for i in range(2, count, 2)] + [(i, i + 1) for i in range(1, count - 1, 2)]
    sent = lax.ppermute(lax.dynamic_slice_in_dim(cells, side, 1, axis=2), "gz", pairs)
    even = side == 0
    below = jnp.where(even, sent, partner_face)
    above = jnp.where(even, partner_face, sent)
    size = cells.shape[2]
    minus = jnp.concatenate([below, lax.slice_in_dim(cells, 0, size - 1, axis=2)], axis=2)
    plus = jnp.concatenate([lax.slice_in_dim(cells, 1, size, axis=2), above], axis=2)
    return minus, plus


def from_below(slab, axis):
    count = lax.axis_size(axis)
    return lax.ppermute(slab, axis, [(i, i + 1) for i in range(count - 1)])


def from_above(slab, axis):
    count = lax.axis_size(axis)
    return lax.ppermute(slab, axis, [(i + 1, i) for i in range(count - 1)])


def faces(cells, axis, dim):
    size = cells.shape[dim]
    first = lax.slice_in_dim(cells, 0, 1, axis=dim)
    last = lax.slice_in_dim(cells, size - 1, size, axis=dim)
    below = jnp.concatenate([from_below(last, axis), lax.slice_in_dim(cells, 0, size - 1, axis=dim)], axis=dim)
    above = jnp.concatenate([lax.slice_in_dim(cells, 1, size, axis=dim), from_above(first, axis)], axis=dim)
    return below, above


def local(coefficients, level_weights, coupling, positions, block_leaf, block_count):
    chunks = coefficients.shape[1]
    done, partner_slabs, weights = pipelined(coefficients, level_weights, chunks, positions)
    done[-1], partner_slabs = lax.optimization_barrier((done[-1], partner_slabs))
    cells = jnp.concatenate(done, axis=1)
    partner_face = mix(
        jnp.concatenate([theirs for theirs, _ in partner_slabs], axis=1),
        jnp.concatenate([ours for _, ours in partner_slabs], axis=1),
        level_weights[len(LEVEL_PLAN) - 1],
    )
    minus_x, plus_x = faces(cells, "gx", 0)
    minus_y, plus_y = faces(cells, "gy", 1)
    minus_z, plus_z = z_faces(cells, partner_face)
    neighbours = (minus_x, plus_x, minus_y, plus_y, minus_z, plus_z)
    total = cells.astype(jnp.float32)
    for index in range(6):
        total = total + apply_map(coupling[index], neighbours[index])
    grid = total.astype(jnp.bfloat16)
    return sample(grid, weights, block_leaf, block_count)


def solution(mesh):
    placed = (
        P("gx", "gy", "gz", None, None),
        P(),
        P(),
        P(None, ("gx", "gy", "gz")),
        P(("gx", "gy", "gz")),
        P(("gx", "gy", "gz")),
    )
    return jax.shard_map(
        local, mesh=mesh, in_specs=placed, out_specs=P(("gx", "gy", "gz"), None), check_vma=False
    )
```

```python
import math

import numpy as np
import jax
import jax.numpy as jnp
from jax import lax
from jax.experimental import pallas as pl
from jax.experimental.pallas import tpu as pltpu
from jax.sharding import PartitionSpec as P

PTS = 8
ROWS = 128
BLOCKS_PER_STEP = 8

NODES = [
    float(v)
    for v in np.cos(
        np.float32(math.pi) * (np.float32(2.0) * np.arange(PTS, dtype=np.float32) + np.float32(1.0)) / np.float32(2.0 * PTS)
    ).astype(np.float32)
]


def from_partner(shard, axis, apart):
    return lax.ppermute(shard, axis, [(i, i ^ 1 << apart) for i in range(lax.axis_size(axis))])


def extended(cells, sides, width):
    for axis, dim in sides:
        count = lax.axis_size(axis)
        ends = count - 1
        head = lax.slice_in_dim(cells, 0, width, axis=dim)
        tail = lax.slice_in_dim(cells, cells.shape[dim] - width, cells.shape[dim], axis=dim)
        cells = jnp.concatenate(
            [
                lax.ppermute(tail, axis, [(i, (i + 1) % count) for i in range(ends)]),
                cells,
                lax.ppermute(head, axis, [((i + 1) % count, i) for i in range(ends)]),
            ],
            axis=dim,
        )
    return cells


def swapped(block):
    half = block.shape[-1] // 2
    return jnp.concatenate([-block[..., half:], block[..., :half]], axis=-1)


def apply_map(weights, block):
    return jnp.einsum("jk,...kc->...jc", weights, block, preferred_element_type=jnp.float32)


def mix(block, other, weights):
    total = apply_map(weights[0, 0], block) + apply_map(weights[0, 1], swapped(block))
    total = total + apply_map(weights[1, 0], other) + apply_map(weights[1, 1], swapped(other))
    return total.astype(jnp.bfloat16)


def basis(u, row):
    ub = jnp.broadcast_to(u, (PTS, ROWS))
    tcol = jnp.zeros((PTS, ROWS), jnp.float32)
    for j in range(PTS):
        tcol = jnp.where(row == j, NODES[j], tcol)
    term = jnp.ones((PTS, ROWS), jnp.float32)
    for m in range(PTS):
        own = row == m
        num = jnp.where(own, 1.0, ub - NODES[m])
        den = jnp.where(own, 1.0, tcol - NODES[m])
        term = term * num / den
    return term


def sample_kernel(leaf_ref, count_ref, pos_ref, grid_ref, out_ref):
    step = pl.program_id(0)
    row = lax.broadcasted_iota(jnp.int32, (PTS, ROWS), 0)
    live_row = lax.broadcasted_iota(jnp.int32, (ROWS, out_ref.shape[1]), 0)
    for i in range(BLOCKS_PER_STEP):
        b = step * BLOCKS_PER_STEP + i
        u = pos_ref[:, i * ROWS:(i + 1) * ROWS]
        lx = basis(u[0:1, :], row)
        ly = basis(u[1:2, :], row)
        lz = basis(u[2:3, :], row)
        pieces = []
        for jx in range(PTS):
            bx = jnp.broadcast_to(lx[jx:jx + 1, :], (PTS, ROWS))
            for jy in range(PTS):
                by = jnp.broadcast_to(ly[jy:jy + 1, :], (PTS, ROWS))
                pieces.append((bx * by) * lz)
        weights_t = jnp.concatenate(pieces, axis=0).astype(jnp.bfloat16)
        leaf = leaf_ref[b]
        place = ((leaf // 2) % 4) * 4 + (leaf // 8) * 2 + leaf % 2
        values = jnp.dot(grid_ref[place], weights_t, preferred_element_type=jnp.float32).T
        values = jnp.where(live_row < count_ref[b], values, 0.0)
        out_ref[i * ROWS:(i + 1) * ROWS, :] = values.astype(out_ref.dtype)


def sample(grid, positions, block_leaf, block_count):
    lx, ly, lz, cheb, cols = grid.shape
    leaf_grid = jnp.transpose(grid, (1, 0, 2, 4, 3)).reshape(ly * lx * lz, cols, cheb)
    blocks = block_leaf.shape[0]
    width = BLOCKS_PER_STEP * ROWS
    spec = pltpu.PrefetchScalarGridSpec(
        num_scalar_prefetch=2,
        grid=(blocks // BLOCKS_PER_STEP,),
        in_specs=[
            pl.BlockSpec((3, width), lambda s, lf, ct: (0, s)),
            pl.BlockSpec((lx * ly * lz, cols, cheb), lambda s, lf, ct: (0, 0, 0)),
        ],
        out_specs=pl.BlockSpec((width, cols), lambda s, lf, ct: (s, 0)),
    )
    return pl.pallas_call(
        sample_kernel,
        grid_spec=spec,
        out_shape=jax.ShapeDtypeStruct((blocks * ROWS, cols), jnp.bfloat16),
    )(block_leaf, block_count, positions, leaf_grid)


def butterfly(cells, level_weights):
    for level in range(2):
        cells = mix(cells, from_partner(cells, "gx", level), level_weights[level])
    cells = mix(cells, from_partner(cells, "gy", 0), level_weights[2])
    return mix(cells, from_partner(cells, "gz", 0), level_weights[3])


LEVEL_PLAN = (("gx", 0), ("gx", 1), ("gy", 0), ("gz", 0))


def pipelined(coefficients, level_weights, chunks):
    cells = [coefficients[:, k:k + 1] for k in range(chunks)]
    partner_faces = [None] * chunks
    levels = len(LEVEL_PLAN)
    side = lax.axis_index("gz") % 2
    for tick in range(chunks + levels - 1):
        active = [k for k in range(chunks) if 0 <= tick - k < levels]
        ready = {}
        for k in active:
            if k > 0 and tick - k + 1 < levels:
                ready[k], _ = lax.optimization_barrier((cells[k], cells[k - 1]))
            else:
                ready[k] = cells[k]
        for k in active:
            level = tick - k
            axis, bit = LEVEL_PLAN[level]
            block = ready[k]
            other = from_partner(block, axis, bit)
            cells[k] = mix(block, other, level_weights[level])
            if level == levels - 1:
                partner_faces[k] = (
                    lax.dynamic_slice_in_dim(other, side, 1, axis=2),
                    lax.dynamic_slice_in_dim(block, side, 1, axis=2),
                )
    return cells, partner_faces


def z_faces(cells, partner_face):
    count = lax.axis_size("gz")
    side = lax.axis_index("gz") % 2
    pairs = [(i, i - 1) for i in range(2, count, 2)] + [(i, i + 1) for i in range(1, count - 1, 2)]
    sent = lax.ppermute(lax.dynamic_slice_in_dim(cells, side, 1, axis=2), "gz", pairs)
    even = side == 0
    below = jnp.where(even, sent, partner_face)
    above = jnp.where(even, partner_face, sent)
    size = cells.shape[2]
    minus = jnp.concatenate([below, lax.slice_in_dim(cells, 0, size - 1, axis=2)], axis=2)
    plus = jnp.concatenate([lax.slice_in_dim(cells, 1, size, axis=2), above], axis=2)
    return minus, plus


def from_below(slab, axis):
    count = lax.axis_size(axis)
    return lax.ppermute(slab, axis, [(i, i + 1) for i in range(count - 1)])


def from_above(slab, axis):
    count = lax.axis_size(axis)
    return lax.ppermute(slab, axis, [(i + 1, i) for i in range(count - 1)])


def faces(cells, axis, dim):
    size = cells.shape[dim]
    first = lax.slice_in_dim(cells, 0, 1, axis=dim)
    last = lax.slice_in_dim(cells, size - 1, size, axis=dim)
    below = jnp.concatenate([from_below(last, axis), lax.slice_in_dim(cells, 0, size - 1, axis=dim)], axis=dim)
    above = jnp.concatenate([lax.slice_in_dim(cells, 1, size, axis=dim), from_above(first, axis)], axis=dim)
    return below, above


def local(coefficients, level_weights, coupling, positions, block_leaf, block_count):
    chunks = coefficients.shape[1]
    done, partner_slabs = pipelined(coefficients, level_weights, chunks)
    done[-1], partner_slabs = lax.optimization_barrier((done[-1], partner_slabs))
    cells = jnp.concatenate(done, axis=1)
    partner_face = mix(
        jnp.concatenate([theirs for theirs, _ in partner_slabs], axis=1),
        jnp.concatenate([ours for _, ours in partner_slabs], axis=1),
        level_weights[len(LEVEL_PLAN) - 1],
    )
    minus_x, plus_x = faces(cells, "gx", 0)
    minus_y, plus_y = faces(cells, "gy", 1)
    minus_z, plus_z = z_faces(cells, partner_face)
    neighbours = (minus_x, plus_x, minus_y, plus_y, minus_z, plus_z)
    total = cells.astype(jnp.float32)
    for index in range(6):
        total = total + apply_map(coupling[index], neighbours[index])
    grid = total.astype(jnp.bfloat16)
    return sample(grid, positions, block_leaf, block_count)


def solution(mesh):
    placed = (
        P("gx", "gy", "gz", None, None),
        P(),
        P(),
        P(None, ("gx", "gy", "gz")),
        P(("gx", "gy", "gz")),
        P(("gx", "gy", "gz")),
    )
    return jax.shard_map(
        local, mesh=mesh, in_specs=placed, out_specs=P(("gx", "gy", "gz"), None), check_vma=False
    )
```

```python
import math

import numpy as np
import jax
import jax.numpy as jnp
from jax import lax
from jax.experimental import pallas as pl
from jax.experimental.pallas import tpu as pltpu
from jax.sharding import PartitionSpec as P

PTS = 8
ROWS = 128
BLOCKS_PER_STEP = 8

NODES = [
    float(v)
    for v in np.cos(
        np.float32(math.pi) * (np.float32(2.0) * np.arange(PTS, dtype=np.float32) + np.float32(1.0)) / np.float32(2.0 * PTS)
    ).astype(np.float32)
]


def from_partner(shard, axis, apart):
    return lax.ppermute(shard, axis, [(i, i ^ 1 << apart) for i in range(lax.axis_size(axis))])


def swapped(block):
    half = block.shape[-1] // 2
    return jnp.concatenate([-block[..., half:], block[..., :half]], axis=-1)


def apply_map(weights, block):
    return jnp.einsum("jk,...kc->...jc", weights, block, preferred_element_type=jnp.float32)


def mix(block, other, weights):
    plain = apply_map(weights[0, 0], block) + apply_map(weights[1, 0], other)
    turned = apply_map(weights[0, 1], block) + apply_map(weights[1, 1], other)
    return (plain + swapped(turned)).astype(jnp.bfloat16)


def basis(u, row):
    ub = jnp.broadcast_to(u, (PTS, ROWS))
    tcol = jnp.zeros((PTS, ROWS), jnp.float32)
    for j in range(PTS):
        tcol = jnp.where(row == j, NODES[j], tcol)
    term = jnp.ones((PTS, ROWS), jnp.float32)
    for m in range(PTS):
        own = row == m
        num = jnp.where(own, 1.0, ub - NODES[m])
        den = jnp.where(own, 1.0, tcol - NODES[m])
        term = term * num / den
    return term


def sample_kernel(leaf_ref, count_ref, pos_ref, grid_ref, out_ref):
    step = pl.program_id(0)
    row = lax.broadcasted_iota(jnp.int32, (PTS, ROWS), 0)
    live_row = lax.broadcasted_iota(jnp.int32, (ROWS, out_ref.shape[1]), 0)

    def one_block(i, carry):
        b = step * BLOCKS_PER_STEP + i
        start = pl.multiple_of(i * ROWS, ROWS)
        u = pos_ref[:, pl.ds(start, ROWS)]
        lx = basis(u[0:1, :], row)
        ly = basis(u[1:2, :], row)
        lz = basis(u[2:3, :], row)
        pieces = []
        for jx in range(PTS):
            bx = jnp.broadcast_to(lx[jx:jx + 1, :], (PTS, ROWS))
            for jy in range(PTS):
                by = jnp.broadcast_to(ly[jy:jy + 1, :], (PTS, ROWS))
                pieces.append((bx * by) * lz)
        weights_t = jnp.concatenate(pieces, axis=0).astype(jnp.bfloat16)
        leaf = leaf_ref[b]
        place = ((leaf // 2) % 4) * 4 + (leaf // 8) * 2 + leaf % 2
        values = jnp.dot(grid_ref[place], weights_t, preferred_element_type=jnp.float32).T
        values = jnp.where(live_row < count_ref[b], values, 0.0)
        out_ref[pl.ds(start, ROWS), :] = values.astype(out_ref.dtype)
        return carry

    lax.fori_loop(0, BLOCKS_PER_STEP, one_block, 0)


def sample(grid, positions, block_leaf, block_count):
    lx, ly, lz, cheb, cols = grid.shape
    leaf_grid = jnp.transpose(grid, (1, 0, 2, 4, 3)).reshape(ly * lx * lz, cols, cheb)
    blocks = block_leaf.shape[0]
    width = BLOCKS_PER_STEP * ROWS
    spec = pltpu.PrefetchScalarGridSpec(
        num_scalar_prefetch=2,
        grid=(blocks // BLOCKS_PER_STEP,),
        in_specs=[
            pl.BlockSpec((3, width), lambda s, lf, ct: (0, s)),
            pl.BlockSpec((lx * ly * lz, cols, cheb), lambda s, lf, ct: (0, 0, 0)),
        ],
        out_specs=pl.BlockSpec((width, cols), lambda s, lf, ct: (s, 0)),
    )
    return pl.pallas_call(
        sample_kernel,
        grid_spec=spec,
        out_shape=jax.ShapeDtypeStruct((blocks * ROWS, cols), jnp.bfloat16),
    )(block_leaf, block_count, positions, leaf_grid)


LEVEL_PLAN = (("gx", 0), ("gx", 1), ("gy", 0), ("gz", 0))


def pipelined(coefficients, level_weights, chunks):
    cells = [coefficients[:, k:k + 1] for k in range(chunks)]
    levels = len(LEVEL_PLAN)
    for tick in range(chunks + levels - 1):
        active = [k for k in range(chunks) if 0 <= tick - k < levels]
        ready = {}
        for k in active:
            if k > 0 and tick - k + 1 < levels:
                ready[k], _ = lax.optimization_barrier((cells[k], cells[k - 1]))
            else:
                ready[k] = cells[k]
        for k in active:
            level = tick - k
            axis, bit = LEVEL_PLAN[level]
            block = ready[k]
            other = from_partner(block, axis, bit)
            cells[k] = mix(block, other, level_weights[level])
    return cells


def from_below(slab, axis):
    count = lax.axis_size(axis)
    return lax.ppermute(slab, axis, [(i, i + 1) for i in range(count - 1)])


def from_above(slab, axis):
    count = lax.axis_size(axis)
    return lax.ppermute(slab, axis, [(i + 1, i) for i in range(count - 1)])


def faces(cells, axis, dim):
    size = cells.shape[dim]
    first = lax.slice_in_dim(cells, 0, 1, axis=dim)
    last = lax.slice_in_dim(cells, size - 1, size, axis=dim)
    below = jnp.concatenate([from_below(last, axis), lax.slice_in_dim(cells, 0, size - 1, axis=dim)], axis=dim)
    above = jnp.concatenate([lax.slice_in_dim(cells, 1, size, axis=dim), from_above(first, axis)], axis=dim)
    return below, above


def local(coefficients, level_weights, coupling, positions, block_leaf, block_count):
    chunks = coefficients.shape[1]
    cells = jnp.concatenate(pipelined(coefficients, level_weights, chunks), axis=1)
    minus_x, plus_x = faces(cells, "gx", 0)
    minus_y, plus_y = faces(cells, "gy", 1)
    minus_z, plus_z = faces(cells, "gz", 2)
    neighbours = (minus_x, plus_x, minus_y, plus_y, minus_z, plus_z)
    total = cells.astype(jnp.float32)
    for index in range(6):
        total = total + apply_map(coupling[index], neighbours[index])
    grid = total.astype(jnp.bfloat16)
    return sample(grid, positions, block_leaf, block_count)


def solution(mesh):
    placed = (
        P("gx", "gy", "gz", None, None),
        P(),
        P(),
        P(None, ("gx", "gy", "gz")),
        P(("gx", "gy", "gz")),
        P(("gx", "gy", "gz")),
    )
    return jax.shard_map(
        local, mesh=mesh, in_specs=placed, out_specs=P(("gx", "gy", "gz"), None), check_vma=False
    )
```

```python
import math

import numpy as np
import jax
import jax.numpy as jnp
from jax import lax
from jax.experimental import pallas as pl
from jax.experimental.pallas import tpu as pltpu
from jax.sharding import PartitionSpec as P

PTS = 8
ROWS = 128
BLOCKS_PER_STEP = 8

NODES = [
    float(v)
    for v in np.cos(
        np.float32(math.pi) * (np.float32(2.0) * np.arange(PTS, dtype=np.float32) + np.float32(1.0)) / np.float32(2.0 * PTS)
    ).astype(np.float32)
]


def from_partner(shard, axis, apart):
    return lax.ppermute(shard, axis, [(i, i ^ 1 << apart) for i in range(lax.axis_size(axis))])


def swapped(block):
    half = block.shape[-1] // 2
    return jnp.concatenate([-block[..., half:], block[..., :half]], axis=-1)


def apply_map(weights, block):
    return jnp.einsum("jk,...kc->...jc", weights, block, preferred_element_type=jnp.float32)


def mix(block, other, weights):
    plain = apply_map(weights[0, 0], block) + apply_map(weights[1, 0], other)
    turned = apply_map(weights[0, 1], block) + apply_map(weights[1, 1], other)
    return (plain + swapped(turned)).astype(jnp.bfloat16)


def basis(u, row):
    ub = jnp.broadcast_to(u, (PTS, ROWS))
    tcol = jnp.zeros((PTS, ROWS), jnp.float32)
    for j in range(PTS):
        tcol = jnp.where(row == j, NODES[j], tcol)
    term = jnp.ones((PTS, ROWS), jnp.float32)
    for m in range(PTS):
        own = row == m
        num = jnp.where(own, 1.0, ub - NODES[m])
        den = jnp.where(own, 1.0, tcol - NODES[m])
        term = term * num / den
    return term


def sample_kernel(leaf_ref, count_ref, pos_ref, grid_ref, out_ref):
    step = pl.program_id(0)
    row = lax.broadcasted_iota(jnp.int32, (PTS, ROWS), 0)
    live_row = lax.broadcasted_iota(jnp.int32, (ROWS, out_ref.shape[1]), 0)
    for i in range(BLOCKS_PER_STEP):
        b = step * BLOCKS_PER_STEP + i
        u = pos_ref[:, i * ROWS:(i + 1) * ROWS]
        lx = basis(u[0:1, :], row)
        ly = basis(u[1:2, :], row)
        lz = basis(u[2:3, :], row)
        pieces = []
        for jx in range(PTS):
            bx = jnp.broadcast_to(lx[jx:jx + 1, :], (PTS, ROWS))
            for jy in range(PTS):
                by = jnp.broadcast_to(ly[jy:jy + 1, :], (PTS, ROWS))
                pieces.append((bx * by) * lz)
        weights_t = jnp.concatenate(pieces, axis=0).astype(jnp.bfloat16)
        leaf = leaf_ref[b]
        place = ((leaf // 2) % 4) * 4 + (leaf // 8) * 2 + leaf % 2
        values = jnp.dot(grid_ref[place], weights_t, preferred_element_type=jnp.float32).T
        values = jnp.where(live_row < count_ref[b], values, 0.0)
        out_ref[i * ROWS:(i + 1) * ROWS, :] = values.astype(out_ref.dtype)


def sample(grid, positions, block_leaf, block_count):
    lx, ly, lz, cheb, cols = grid.shape
    leaf_grid = jnp.transpose(grid, (1, 0, 2, 4, 3)).reshape(ly * lx * lz, cols, cheb)
    blocks = block_leaf.shape[0]
    width = BLOCKS_PER_STEP * ROWS
    spec = pltpu.PrefetchScalarGridSpec(
        num_scalar_prefetch=2,
        grid=(blocks // BLOCKS_PER_STEP,),
        in_specs=[
            pl.BlockSpec((3, width), lambda s, lf, ct: (0, s)),
            pl.BlockSpec((lx * ly * lz, cols, cheb), lambda s, lf, ct: (0, 0, 0)),
        ],
        out_specs=pl.BlockSpec((width, cols), lambda s, lf, ct: (s, 0)),
    )
    return pl.pallas_call(
        sample_kernel,
        grid_spec=spec,
        out_shape=jax.ShapeDtypeStruct((blocks * ROWS, cols), jnp.bfloat16),
    )(block_leaf, block_count, positions, leaf_grid)


LEVEL_PLAN = (("gx", 0), ("gx", 1), ("gy", 0), ("gz", 0))


def pipelined(coefficients, level_weights, chunks):
    cells = [coefficients[:, k:k + 1] for k in range(chunks)]
    levels = len(LEVEL_PLAN)
    for tick in range(chunks + levels - 1):
        active = [k for k in range(chunks) if 0 <= tick - k < levels]
        ready = {}
        for k in active:
            if k > 0 and tick - k + 1 < levels:
                ready[k], _ = lax.optimization_barrier((cells[k], cells[k - 1]))
            else:
                ready[k] = cells[k]
        for k in active:
            level = tick - k
            axis, bit = LEVEL_PLAN[level]
            block = ready[k]
            other = from_partner(block, axis, bit)
            cells[k] = mix(block, other, level_weights[level])
    return cells


def from_below(slab, axis):
    count = lax.axis_size(axis)
    return lax.ppermute(slab, axis, [(i, i + 1) for i in range(count - 1)])


def from_above(slab, axis):
    count = lax.axis_size(axis)
    return lax.ppermute(slab, axis, [(i + 1, i) for i in range(count - 1)])


def faces(cells, axis, dim):
    size = cells.shape[dim]
    first = lax.slice_in_dim(cells, 0, 1, axis=dim)
    last = lax.slice_in_dim(cells, size - 1, size, axis=dim)
    below = jnp.concatenate([from_below(last, axis), lax.slice_in_dim(cells, 0, size - 1, axis=dim)], axis=dim)
    above = jnp.concatenate([lax.slice_in_dim(cells, 1, size, axis=dim), from_above(first, axis)], axis=dim)
    return below, above


def local(coefficients, level_weights, coupling, positions, block_leaf, block_count):
    chunks = coefficients.shape[1]
    cells = jnp.concatenate(pipelined(coefficients, level_weights, chunks), axis=1)
    minus_x, plus_x = faces(cells, "gx", 0)
    minus_y, plus_y = faces(cells, "gy", 1)
    minus_z, plus_z = faces(cells, "gz", 2)
    neighbours = (minus_x, plus_x, minus_y, plus_y, minus_z, plus_z)
    total = cells.astype(jnp.float32)
    for index in range(6):
        total = total + apply_map(coupling[index], neighbours[index])
    grid = total.astype(jnp.bfloat16)
    return sample(grid, positions, block_leaf, block_count)


def solution(mesh):
    placed = (
        P("gx", "gy", "gz", None, None),
        P(),
        P(),
        P(None, ("gx", "gy", "gz")),
        P(("gx", "gy", "gz")),
        P(("gx", "gy", "gz")),
    )
    return jax.shard_map(
        local, mesh=mesh, in_specs=placed, out_specs=P(("gx", "gy", "gz"), None), check_vma=False
    )
```

```python
import math

import numpy as np
import jax
import jax.numpy as jnp
from jax import lax
from jax.experimental import pallas as pl
from jax.experimental.pallas import tpu as pltpu
from jax.sharding import PartitionSpec as P

PTS = 8
ROWS = 128
BLOCKS_PER_STEP = 8

NODES = [
    float(v)
    for v in np.cos(
        np.float32(math.pi) * (np.float32(2.0) * np.arange(PTS, dtype=np.float32) + np.float32(1.0)) / np.float32(2.0 * PTS)
    ).astype(np.float32)
]


def from_partner(shard, axis, apart):
    return lax.ppermute(shard, axis, [(i, i ^ 1 << apart) for i in range(lax.axis_size(axis))])


def swapped(block):
    half = block.shape[-1] // 2
    return jnp.concatenate([-block[..., half:], block[..., :half]], axis=-1)


def apply_map(weights, block):
    return jnp.einsum("jk,...kc->...jc", weights, block, preferred_element_type=jnp.float32)


def mix(block, other, weights):
    plain = apply_map(weights[0, 0], block) + apply_map(weights[1, 0], other)
    turned = apply_map(weights[0, 1], block) + apply_map(weights[1, 1], other)
    return (plain + swapped(turned)).astype(jnp.bfloat16)


def basis(u, row):
    ub = jnp.broadcast_to(u, (PTS, ROWS))
    tcol = jnp.zeros((PTS, ROWS), jnp.float32)
    for j in range(PTS):
        tcol = jnp.where(row == j, NODES[j], tcol)
    term = jnp.ones((PTS, ROWS), jnp.float32)
    for m in range(PTS):
        own = row == m
        num = jnp.where(own, 1.0, ub - NODES[m])
        den = jnp.where(own, 1.0, tcol - NODES[m])
        term = term * num / den
    return term


def sample_kernel(leaf_ref, count_ref, pos_ref, grid_ref, out_ref):
    step = pl.program_id(0)
    row = lax.broadcasted_iota(jnp.int32, (PTS, ROWS), 0)
    live_row = lax.broadcasted_iota(jnp.int32, (ROWS, out_ref.shape[1]), 0)
    for i in range(BLOCKS_PER_STEP):
        b = step * BLOCKS_PER_STEP + i
        u = pos_ref[:, i * ROWS:(i + 1) * ROWS]
        lx = basis(u[0:1, :], row)
        ly = basis(u[1:2, :], row)
        lz = basis(u[2:3, :], row)
        pieces = []
        for jx in range(PTS):
            bx = jnp.broadcast_to(lx[jx:jx + 1, :], (PTS, ROWS))
            for jy in range(PTS):
                by = jnp.broadcast_to(ly[jy:jy + 1, :], (PTS, ROWS))
                pieces.append((bx * by) * lz)
        weights_t = jnp.concatenate(pieces, axis=0).astype(jnp.bfloat16)
        leaf = leaf_ref[b]
        place = ((leaf // 2) % 4) * 4 + (leaf // 8) * 2 + leaf % 2
        values = jnp.dot(grid_ref[place], weights_t, preferred_element_type=jnp.float32).T
        values = jnp.where(live_row < count_ref[b], values, 0.0)
        out_ref[i * ROWS:(i + 1) * ROWS, :] = values.astype(out_ref.dtype)


def sample(leaf_grid, positions, block_leaf, block_count):
    leaves, cols, cheb = leaf_grid.shape
    blocks = block_leaf.shape[0]
    width = BLOCKS_PER_STEP * ROWS
    spec = pltpu.PrefetchScalarGridSpec(
        num_scalar_prefetch=2,
        grid=(blocks // BLOCKS_PER_STEP,),
        in_specs=[
            pl.BlockSpec((3, width), lambda s, lf, ct: (0, s)),
            pl.BlockSpec((leaves, cols, cheb), lambda s, lf, ct: (0, 0, 0)),
        ],
        out_specs=pl.BlockSpec((width, cols), lambda s, lf, ct: (s, 0)),
    )
    return pl.pallas_call(
        sample_kernel,
        grid_spec=spec,
        out_shape=jax.ShapeDtypeStruct((blocks * ROWS, cols), jnp.bfloat16),
    )(block_leaf, block_count, positions, leaf_grid)


LEVEL_PLAN = (("gx", 0), ("gx", 1), ("gy", 0), ("gz", 0))


def pipelined(coefficients, level_weights, chunks):
    cells = [coefficients[:, k:k + 1] for k in range(chunks)]
    partner_faces = [None] * chunks
    levels = len(LEVEL_PLAN)
    side = lax.axis_index("gz") % 2
    for tick in range(chunks + levels - 1):
        active = [k for k in range(chunks) if 0 <= tick - k < levels]
        ready = {}
        for k in active:
            if k > 0 and tick - k + 1 < levels:
                ready[k], _ = lax.optimization_barrier((cells[k], cells[k - 1]))
            else:
                ready[k] = cells[k]
        for k in active:
            level = tick - k
            axis, bit = LEVEL_PLAN[level]
            block = ready[k]
            other = from_partner(block, axis, bit)
            cells[k] = mix(block, other, level_weights[level])
            if level == levels - 1:
                partner_faces[k] = (
                    lax.dynamic_slice_in_dim(other, side, 1, axis=2),
                    lax.dynamic_slice_in_dim(block, side, 1, axis=2),
                )
    return cells, partner_faces


def from_below(slab, axis):
    count = lax.axis_size(axis)
    return lax.ppermute(slab, axis, [(i, i + 1) for i in range(count - 1)])


def from_above(slab, axis):
    count = lax.axis_size(axis)
    return lax.ppermute(slab, axis, [(i + 1, i) for i in range(count - 1)])


def z_faces(cells, partner_face):
    count = lax.axis_size("gz")
    side = lax.axis_index("gz") % 2
    pairs = [(i, i - 1) for i in range(2, count, 2)] + [(i, i + 1) for i in range(1, count - 1, 2)]
    sent = lax.ppermute(lax.dynamic_slice_in_dim(cells, side, 1, axis=2), "gz", pairs)
    even = side == 0
    return jnp.where(even, sent, partner_face), jnp.where(even, partner_face, sent)


def coupling_kernel(weight_ref, prev_ref, cell_ref, next_ref, xb_ref, xa_ref, yb_ref, ya_ref, zb_ref, za_ref, out_ref):
    y = pl.program_id(0)
    last = pl.num_programs(0) - 1

    def coupled(block, index):
        return lax.dot_general(
            block, weight_ref[index], (((1,), (1,)), ((), ())), preferred_element_type=jnp.float32
        )

    for x in range(2):
        for z in range(2):
            own = cell_ref[0, x, z]
            total = own.astype(jnp.float32)
            total = total + coupled(xb_ref[0, 0, z] if x == 0 else cell_ref[0, 0, z], 0)
            total = total + coupled(cell_ref[0, 1, z] if x == 0 else xa_ref[0, 0, z], 1)
            total = total + coupled(jnp.where(y == 0, yb_ref[0, x, z], prev_ref[0, x, z]), 2)
            total = total + coupled(jnp.where(y == last, ya_ref[0, x, z], next_ref[0, x, z]), 3)
            total = total + coupled(zb_ref[0, x, 0] if z == 0 else cell_ref[0, x, 0], 4)
            total = total + coupled(cell_ref[0, x, 1] if z == 0 else za_ref[0, x, 0], 5)
            out_ref[0, x, z] = total.astype(out_ref.dtype)


def couple(coupling, cells, xb, xa, yb, ya, zb, za):
    def turned(a):
        return jnp.transpose(a, (1, 0, 2, 4, 3))

    lx, ly, lz, cheb, cols = cells.shape
    leaf = (1, lx, lz, cols, cheb)
    weight_spec = pl.BlockSpec(coupling.shape, lambda y: (0, 0, 0))
    specs = [
        weight_spec,
        pl.BlockSpec(leaf, lambda y: (jnp.maximum(y - 1, 0), 0, 0, 0, 0)),
        pl.BlockSpec(leaf, lambda y: (y, 0, 0, 0, 0)),
        pl.BlockSpec(leaf, lambda y: (jnp.minimum(y + 1, ly - 1), 0, 0, 0, 0)),
        pl.BlockSpec((1, 1, lz, cols, cheb), lambda y: (y, 0, 0, 0, 0)),
        pl.BlockSpec((1, 1, lz, cols, cheb), lambda y: (y, 0, 0, 0, 0)),
        pl.BlockSpec(leaf, lambda y: (0, 0, 0, 0, 0)),
        pl.BlockSpec(leaf, lambda y: (0, 0, 0, 0, 0)),
        pl.BlockSpec((1, lx, 1, cols, cheb), lambda y: (y, 0, 0, 0, 0)),
        pl.BlockSpec((1, lx, 1, cols, cheb), lambda y: (y, 0, 0, 0, 0)),
    ]
    cells_t = turned(cells)
    out = pl.pallas_call(
        coupling_kernel,
        grid=(ly,),
        in_specs=specs,
        out_specs=pl.BlockSpec(leaf, lambda y: (y, 0, 0, 0, 0)),
        out_shape=jax.ShapeDtypeStruct((ly, lx, lz, cols, cheb), jnp.bfloat16),
    )(coupling, cells_t, cells_t, cells_t, turned(xb), turned(xa), turned(yb), turned(ya), turned(zb), turned(za))
    return out.reshape(ly * lx * lz, cols, cheb)


def local(coefficients, level_weights, coupling, positions, block_leaf, block_count):
    chunks = coefficients.shape[1]
    done, partner_slabs = pipelined(coefficients, level_weights, chunks)
    done[-1], partner_slabs = lax.optimization_barrier((done[-1], partner_slabs))
    cells = jnp.concatenate(done, axis=1)
    partner_face = mix(
        jnp.concatenate([theirs for theirs, _ in partner_slabs], axis=1),
        jnp.concatenate([ours for _, ours in partner_slabs], axis=1),
        level_weights[len(LEVEL_PLAN) - 1],
    )
    xb = from_below(cells[cells.shape[0] - 1:], "gx")
    xa = from_above(cells[:1], "gx")
    yb = from_below(cells[:, cells.shape[1] - 1:], "gy")
    ya = from_above(cells[:, :1], "gy")
    zb, za = z_faces(cells, partner_face)
    leaf_grid = couple(coupling, cells, xb, xa, yb, ya, zb, za)
    return sample(leaf_grid, positions, block_leaf, block_count)


def solution(mesh):
    placed = (
        P("gx", "gy", "gz", None, None),
        P(),
        P(),
        P(None, ("gx", "gy", "gz")),
        P(("gx", "gy", "gz")),
        P(("gx", "gy", "gz")),
    )
    return jax.shard_map(
        local, mesh=mesh, in_specs=placed, out_specs=P(("gx", "gy", "gz"), None), check_vma=False
    )
```

```python
import math

import numpy as np
import jax
import jax.numpy as jnp
from jax import lax
from jax.experimental import pallas as pl
from jax.experimental.pallas import tpu as pltpu
from jax.sharding import PartitionSpec as P

PTS = 8
ROWS = 128
BLOCKS_PER_STEP = 8

NODES = [
    float(v)
    for v in np.cos(
        np.float32(math.pi) * (np.float32(2.0) * np.arange(PTS, dtype=np.float32) + np.float32(1.0)) / np.float32(2.0 * PTS)
    ).astype(np.float32)
]


def from_partner(shard, axis, apart):
    return lax.ppermute(shard, axis, [(i, i ^ 1 << apart) for i in range(lax.axis_size(axis))])


def swapped(block):
    half = block.shape[-1] // 2
    return jnp.concatenate([-block[..., half:], block[..., :half]], axis=-1)


def apply_map(weights, block):
    return jnp.einsum("jk,...kc->...jc", weights, block, preferred_element_type=jnp.float32)


def mix(block, other, weights):
    plain = apply_map(weights[0, 0], block) + apply_map(weights[1, 0], other)
    turned = apply_map(weights[0, 1], block) + apply_map(weights[1, 1], other)
    return (plain + swapped(turned)).astype(jnp.bfloat16)


def basis(u, row):
    ub = jnp.broadcast_to(u, (PTS, ROWS))
    tcol = jnp.zeros((PTS, ROWS), jnp.float32)
    for j in range(PTS):
        tcol = jnp.where(row == j, NODES[j], tcol)
    term = jnp.ones((PTS, ROWS), jnp.float32)
    for m in range(PTS):
        own = row == m
        num = jnp.where(own, 1.0, ub - NODES[m])
        den = jnp.where(own, 1.0, tcol - NODES[m])
        term = term * num / den
    return term


def sample_kernel(leaf_ref, count_ref, pos_ref, grid_ref, out_ref):
    step = pl.program_id(0)
    row = lax.broadcasted_iota(jnp.int32, (PTS, ROWS), 0)
    live_row = lax.broadcasted_iota(jnp.int32, (ROWS, out_ref.shape[1]), 0)
    for i in range(BLOCKS_PER_STEP):
        b = step * BLOCKS_PER_STEP + i
        u = pos_ref[:, i * ROWS:(i + 1) * ROWS]
        lx = basis(u[0:1, :], row)
        ly = basis(u[1:2, :], row)
        lz = basis(u[2:3, :], row)
        pieces = []
        for jx in range(PTS):
            bx = jnp.broadcast_to(lx[jx:jx + 1, :], (PTS, ROWS))
            for jy in range(PTS):
                by = jnp.broadcast_to(ly[jy:jy + 1, :], (PTS, ROWS))
                pieces.append((bx * by) * lz)
        weights_t = jnp.concatenate(pieces, axis=0).astype(jnp.bfloat16)
        leaf = leaf_ref[b]
        place = ((leaf // 2) % 4) * 4 + (leaf // 8) * 2 + leaf % 2
        values = jnp.dot(grid_ref[place], weights_t, preferred_element_type=jnp.float32).T
        values = jnp.where(live_row < count_ref[b], values, 0.0)
        out_ref[i * ROWS:(i + 1) * ROWS, :] = values.astype(out_ref.dtype)


def sample(leaf_grid, positions, block_leaf, block_count):
    leaves, cols, cheb = leaf_grid.shape
    blocks = block_leaf.shape[0]
    width = BLOCKS_PER_STEP * ROWS
    spec = pltpu.PrefetchScalarGridSpec(
        num_scalar_prefetch=2,
        grid=(blocks // BLOCKS_PER_STEP,),
        in_specs=[
            pl.BlockSpec((3, width), lambda s, lf, ct: (0, s)),
            pl.BlockSpec((leaves, cols, cheb), lambda s, lf, ct: (0, 0, 0)),
        ],
        out_specs=pl.BlockSpec((width, cols), lambda s, lf, ct: (s, 0)),
    )
    return pl.pallas_call(
        sample_kernel,
        grid_spec=spec,
        out_shape=jax.ShapeDtypeStruct((blocks * ROWS, cols), jnp.bfloat16),
    )(block_leaf, block_count, positions, leaf_grid)


LEVEL_PLAN = (("gx", 0), ("gx", 1), ("gy", 0), ("gz", 0))


def pipelined(coefficients, level_weights, chunks):
    cells = [coefficients[:, k:k + 1] for k in range(chunks)]
    partner_faces = [None] * chunks
    levels = len(LEVEL_PLAN)
    side = lax.axis_index("gz") % 2
    for tick in range(chunks + levels - 1):
        active = [k for k in range(chunks) if 0 <= tick - k < levels]
        ready = {}
        for k in active:
            if k > 0 and tick - k + 1 < levels:
                ready[k], _ = lax.optimization_barrier((cells[k], cells[k - 1]))
            else:
                ready[k] = cells[k]
        for k in active:
            level = tick - k
            axis, bit = LEVEL_PLAN[level]
            block = ready[k]
            other = from_partner(block, axis, bit)
            cells[k] = mix(block, other, level_weights[level])
            if level == levels - 1:
                partner_faces[k] = (
                    lax.dynamic_slice_in_dim(other, side, 1, axis=2),
                    lax.dynamic_slice_in_dim(block, side, 1, axis=2),
                )
    return cells, partner_faces


def from_below(slab, axis):
    count = lax.axis_size(axis)
    return lax.ppermute(slab, axis, [(i, i + 1) for i in range(count - 1)])


def from_above(slab, axis):
    count = lax.axis_size(axis)
    return lax.ppermute(slab, axis, [(i + 1, i) for i in range(count - 1)])


def z_faces(cells, partner_face):
    count = lax.axis_size("gz")
    side = lax.axis_index("gz") % 2
    pairs = [(i, i - 1) for i in range(2, count, 2)] + [(i, i + 1) for i in range(1, count - 1, 2)]
    sent = lax.ppermute(lax.dynamic_slice_in_dim(cells, side, 1, axis=2), "gz", pairs)
    even = side == 0
    return jnp.where(even, sent, partner_face), jnp.where(even, partner_face, sent)


def coupling_kernel(weight_ref, prev_ref, cell_ref, next_ref, xb_ref, xa_ref, yb_ref, ya_ref, zb_ref, za_ref, out_ref):
    y = pl.program_id(0)
    last = pl.num_programs(0) - 1

    def coupled(block, index):
        return jnp.dot(block, weight_ref[index], preferred_element_type=jnp.float32)

    for x in range(2):
        for z in range(2):
            own = cell_ref[0, x, z]
            total = own.astype(jnp.float32)
            total = total + coupled(xb_ref[0, 0, z] if x == 0 else cell_ref[0, 0, z], 0)
            total = total + coupled(cell_ref[0, 1, z] if x == 0 else xa_ref[0, 0, z], 1)
            total = total + coupled(jnp.where(y == 0, yb_ref[0, x, z], prev_ref[0, x, z]), 2)
            total = total + coupled(jnp.where(y == last, ya_ref[0, x, z], next_ref[0, x, z]), 3)
            total = total + coupled(zb_ref[0, x, 0] if z == 0 else cell_ref[0, x, 0], 4)
            total = total + coupled(cell_ref[0, x, 1] if z == 0 else za_ref[0, x, 0], 5)
            out_ref[0, x, z] = total.astype(out_ref.dtype)


def couple(coupling, cells, xb, xa, yb, ya, zb, za):
    def turned(a):
        return jnp.transpose(a, (1, 0, 2, 4, 3))

    lx, ly, lz, cheb, cols = cells.shape
    leaf = (1, lx, lz, cols, cheb)
    weight_spec = pl.BlockSpec(coupling.shape, lambda y: (0, 0, 0))
    specs = [
        weight_spec,
        pl.BlockSpec(leaf, lambda y: (jnp.maximum(y - 1, 0), 0, 0, 0, 0)),
        pl.BlockSpec(leaf, lambda y: (y, 0, 0, 0, 0)),
        pl.BlockSpec(leaf, lambda y: (jnp.minimum(y + 1, ly - 1), 0, 0, 0, 0)),
        pl.BlockSpec((1, 1, lz, cols, cheb), lambda y: (y, 0, 0, 0, 0)),
        pl.BlockSpec((1, 1, lz, cols, cheb), lambda y: (y, 0, 0, 0, 0)),
        pl.BlockSpec(leaf, lambda y: (0, 0, 0, 0, 0)),
        pl.BlockSpec(leaf, lambda y: (0, 0, 0, 0, 0)),
        pl.BlockSpec((1, lx, 1, cols, cheb), lambda y: (y, 0, 0, 0, 0)),
        pl.BlockSpec((1, lx, 1, cols, cheb), lambda y: (y, 0, 0, 0, 0)),
    ]
    cells_t = turned(cells)
    out = pl.pallas_call(
        coupling_kernel,
        grid=(ly,),
        in_specs=specs,
        out_specs=pl.BlockSpec(leaf, lambda y: (y, 0, 0, 0, 0)),
        out_shape=jax.ShapeDtypeStruct((ly, lx, lz, cols, cheb), jnp.bfloat16),
    )(jnp.swapaxes(coupling, 1, 2), cells_t, cells_t, cells_t, turned(xb), turned(xa), turned(yb), turned(ya), turned(zb), turned(za))
    return out.reshape(ly * lx * lz, cols, cheb)


def local(coefficients, level_weights, coupling, positions, block_leaf, block_count):
    chunks = coefficients.shape[1]
    done, partner_slabs = pipelined(coefficients, level_weights, chunks)
    done[-1], partner_slabs = lax.optimization_barrier((done[-1], partner_slabs))
    cells = jnp.concatenate(done, axis=1)
    partner_face = mix(
        jnp.concatenate([theirs for theirs, _ in partner_slabs], axis=1),
        jnp.concatenate([ours for _, ours in partner_slabs], axis=1),
        level_weights[len(LEVEL_PLAN) - 1],
    )
    xb = from_below(cells[cells.shape[0] - 1:], "gx")
    xa = from_above(cells[:1], "gx")
    yb = from_below(cells[:, cells.shape[1] - 1:], "gy")
    ya = from_above(cells[:, :1], "gy")
    zb, za = z_faces(cells, partner_face)
    leaf_grid = couple(coupling, cells, xb, xa, yb, ya, zb, za)
    return sample(leaf_grid, positions, block_leaf, block_count)


def solution(mesh):
    placed = (
        P("gx", "gy", "gz", None, None),
        P(),
        P(),
        P(None, ("gx", "gy", "gz")),
        P(("gx", "gy", "gz")),
        P(("gx", "gy", "gz")),
    )
    return jax.shard_map(
        local, mesh=mesh, in_specs=placed, out_specs=P(("gx", "gy", "gz"), None), check_vma=False
    )
```

```python
import math

import numpy as np
import jax
import jax.numpy as jnp
from jax import lax
from jax.experimental import pallas as pl
from jax.experimental.pallas import tpu as pltpu
from jax.sharding import PartitionSpec as P

PTS = 8
ROWS = 128
BLOCKS_PER_STEP = 8

NODES = [
    float(v)
    for v in np.cos(
        np.float32(math.pi) * (np.float32(2.0) * np.arange(PTS, dtype=np.float32) + np.float32(1.0)) / np.float32(2.0 * PTS)
    ).astype(np.float32)
]


def from_partner(shard, axis, apart):
    return lax.ppermute(shard, axis, [(i, i ^ 1 << apart) for i in range(lax.axis_size(axis))])


def swapped(block):
    half = block.shape[-1] // 2
    return jnp.concatenate([-block[..., half:], block[..., :half]], axis=-1)


def apply_map(weights, block):
    return jnp.einsum("jk,...kc->...jc", weights, block, preferred_element_type=jnp.float32)


def mix(block, other, weights):
    plain = apply_map(weights[0, 0], block) + apply_map(weights[1, 0], other)
    turned = apply_map(weights[0, 1], block) + apply_map(weights[1, 1], other)
    return (plain + swapped(turned)).astype(jnp.bfloat16)


def basis(u, row):
    ub = jnp.broadcast_to(u, (PTS, ROWS))
    tcol = jnp.zeros((PTS, ROWS), jnp.float32)
    for j in range(PTS):
        tcol = jnp.where(row == j, NODES[j], tcol)
    term = jnp.ones((PTS, ROWS), jnp.float32)
    for m in range(PTS):
        own = row == m
        num = jnp.where(own, 1.0, ub - NODES[m])
        den = jnp.where(own, 1.0, tcol - NODES[m])
        term = term * num / den
    return term


def sample_kernel(leaf_ref, count_ref, pos_ref, grid_ref, out_ref):
    step = pl.program_id(0)
    row = lax.broadcasted_iota(jnp.int32, (PTS, ROWS), 0)
    live_row = lax.broadcasted_iota(jnp.int32, (ROWS, out_ref.shape[1]), 0)
    for i in range(BLOCKS_PER_STEP):
        b = step * BLOCKS_PER_STEP + i
        u = pos_ref[:, i * ROWS:(i + 1) * ROWS]
        lx = basis(u[0:1, :], row)
        ly = basis(u[1:2, :], row)
        lz = basis(u[2:3, :], row)
        pieces = []
        for jx in range(PTS):
            bx = jnp.broadcast_to(lx[jx:jx + 1, :], (PTS, ROWS))
            for jy in range(PTS):
                by = jnp.broadcast_to(ly[jy:jy + 1, :], (PTS, ROWS))
                pieces.append((bx * by) * lz)
        weights_t = jnp.concatenate(pieces, axis=0).astype(jnp.bfloat16)
        leaf = leaf_ref[b]
        place = ((leaf // 2) % 4) * 4 + (leaf // 8) * 2 + leaf % 2
        values = jnp.dot(grid_ref[place], weights_t, preferred_element_type=jnp.float32).T
        values = jnp.where(live_row < count_ref[b], values, 0.0)
        out_ref[i * ROWS:(i + 1) * ROWS, :] = values.astype(out_ref.dtype)


def sample(leaf_grid, positions, block_leaf, block_count):
    leaves, cols, cheb = leaf_grid.shape
    blocks = block_leaf.shape[0]
    width = BLOCKS_PER_STEP * ROWS
    spec = pltpu.PrefetchScalarGridSpec(
        num_scalar_prefetch=2,
        grid=(blocks // BLOCKS_PER_STEP,),
        in_specs=[
            pl.BlockSpec((3, width), lambda s, lf, ct: (0, s)),
            pl.BlockSpec((leaves, cols, cheb), lambda s, lf, ct: (0, 0, 0)),
        ],
        out_specs=pl.BlockSpec((width, cols), lambda s, lf, ct: (s, 0)),
    )
    return pl.pallas_call(
        sample_kernel,
        grid_spec=spec,
        out_shape=jax.ShapeDtypeStruct((blocks * ROWS, cols), jnp.bfloat16),
    )(block_leaf, block_count, positions, leaf_grid)


LEVEL_PLAN = (("gx", 0), ("gx", 1), ("gy", 0), ("gz", 0))


def pipelined(coefficients, level_weights, chunks, late):
    cells = [coefficients[:, k:k + 1] for k in range(chunks)]
    partner_faces = [None] * chunks
    levels = len(LEVEL_PLAN)
    side = lax.axis_index("gz") % 2
    for tick in range(chunks + levels - 1):
        active = [k for k in range(chunks) if 0 <= tick - k < levels]
        ready = {}
        for k in active:
            if k > 0 and tick - k + 1 < levels:
                ready[k], _ = lax.optimization_barrier((cells[k], cells[k - 1]))
            else:
                ready[k] = cells[k]
        if tick == chunks + levels - 2:
            late, _ = lax.optimization_barrier((late, ready[active[-1]]))
        for k in active:
            level = tick - k
            axis, bit = LEVEL_PLAN[level]
            block = ready[k]
            other = from_partner(block, axis, bit)
            cells[k] = mix(block, other, level_weights[level])
            if level == levels - 1:
                partner_faces[k] = (
                    lax.dynamic_slice_in_dim(other, side, 1, axis=2),
                    lax.dynamic_slice_in_dim(block, side, 1, axis=2),
                )
    return cells, partner_faces, late


def from_below(slab, axis):
    count = lax.axis_size(axis)
    return lax.ppermute(slab, axis, [(i, i + 1) for i in range(count - 1)])


def from_above(slab, axis):
    count = lax.axis_size(axis)
    return lax.ppermute(slab, axis, [(i + 1, i) for i in range(count - 1)])


def z_faces(cells, partner_face):
    count = lax.axis_size("gz")
    side = lax.axis_index("gz") % 2
    pairs = [(i, i - 1) for i in range(2, count, 2)] + [(i, i + 1) for i in range(1, count - 1, 2)]
    sent = lax.ppermute(lax.dynamic_slice_in_dim(cells, side, 1, axis=2), "gz", pairs)
    even = side == 0
    return jnp.where(even, sent, partner_face), jnp.where(even, partner_face, sent)


def coupling_kernel(weight_ref, prev_ref, cell_ref, next_ref, xb_ref, xa_ref, yb_ref, ya_ref, zb_ref, za_ref, out_ref):
    y = pl.program_id(0)
    last = pl.num_programs(0) - 1

    def coupled(block, index):
        return jnp.dot(block, weight_ref[index], preferred_element_type=jnp.float32)

    for x in range(2):
        for z in range(2):
            own = cell_ref[0, x, z]
            total = own.astype(jnp.float32)
            total = total + coupled(xb_ref[0, 0, z] if x == 0 else cell_ref[0, 0, z], 0)
            total = total + coupled(cell_ref[0, 1, z] if x == 0 else xa_ref[0, 0, z], 1)
            total = total + coupled(jnp.where(y == 0, yb_ref[0, x, z], prev_ref[0, x, z]), 2)
            total = total + coupled(jnp.where(y == last, ya_ref[0, x, z], next_ref[0, x, z]), 3)
            total = total + coupled(zb_ref[0, x, 0] if z == 0 else cell_ref[0, x, 0], 4)
            total = total + coupled(cell_ref[0, x, 1] if z == 0 else za_ref[0, x, 0], 5)
            out_ref[0, x, z] = total.astype(out_ref.dtype)


def couple(coupling, cells, xb, xa, yb, ya, zb, za):
    def turned(a):
        return jnp.transpose(a, (1, 0, 2, 4, 3))

    lx, ly, lz, cheb, cols = cells.shape
    leaf = (1, lx, lz, cols, cheb)
    weight_spec = pl.BlockSpec(coupling.shape, lambda y: (0, 0, 0))
    specs = [
        weight_spec,
        pl.BlockSpec(leaf, lambda y: (jnp.maximum(y - 1, 0), 0, 0, 0, 0)),
        pl.BlockSpec(leaf, lambda y: (y, 0, 0, 0, 0)),
        pl.BlockSpec(leaf, lambda y: (jnp.minimum(y + 1, ly - 1), 0, 0, 0, 0)),
        pl.BlockSpec((1, 1, lz, cols, cheb), lambda y: (y, 0, 0, 0, 0)),
        pl.BlockSpec((1, 1, lz, cols, cheb), lambda y: (y, 0, 0, 0, 0)),
        pl.BlockSpec(leaf, lambda y: (0, 0, 0, 0, 0)),
        pl.BlockSpec(leaf, lambda y: (0, 0, 0, 0, 0)),
        pl.BlockSpec((1, lx, 1, cols, cheb), lambda y: (y, 0, 0, 0, 0)),
        pl.BlockSpec((1, lx, 1, cols, cheb), lambda y: (y, 0, 0, 0, 0)),
    ]
    cells_t = turned(cells)
    out = pl.pallas_call(
        coupling_kernel,
        grid=(ly,),
        in_specs=specs,
        out_specs=pl.BlockSpec(leaf, lambda y: (y, 0, 0, 0, 0)),
        out_shape=jax.ShapeDtypeStruct((ly, lx, lz, cols, cheb), jnp.bfloat16),
    )(coupling, cells_t, cells_t, cells_t, turned(xb), turned(xa), turned(yb), turned(ya), turned(zb), turned(za))
    return out.reshape(ly * lx * lz, cols, cheb)


def local(coefficients, level_weights, coupling, positions, block_leaf, block_count):
    chunks = coefficients.shape[1]
    done, partner_slabs, coupling = pipelined(coefficients, level_weights, chunks, coupling)
    coupling_t = jnp.swapaxes(coupling, 1, 2)
    done[-1], partner_slabs = lax.optimization_barrier((done[-1], partner_slabs))
    cells = jnp.concatenate(done, axis=1)
    partner_face = mix(
        jnp.concatenate([theirs for theirs, _ in partner_slabs], axis=1),
        jnp.concatenate([ours for _, ours in partner_slabs], axis=1),
        level_weights[len(LEVEL_PLAN) - 1],
    )
    xb = from_below(cells[cells.shape[0] - 1:], "gx")
    xa = from_above(cells[:1], "gx")
    yb = from_below(cells[:, cells.shape[1] - 1:], "gy")
    ya = from_above(cells[:, :1], "gy")
    zb, za = z_faces(cells, partner_face)
    leaf_grid = couple(coupling_t, cells, xb, xa, yb, ya, zb, za)
    return sample(leaf_grid, positions, block_leaf, block_count)


def solution(mesh):
    placed = (
        P("gx", "gy", "gz", None, None),
        P(),
        P(),
        P(None, ("gx", "gy", "gz")),
        P(("gx", "gy", "gz")),
        P(("gx", "gy", "gz")),
    )
    return jax.shard_map(
        local, mesh=mesh, in_specs=placed, out_specs=P(("gx", "gy", "gz"), None), check_vma=False
    )
```

```python
import math

import numpy as np
import jax
import jax.numpy as jnp
from jax import lax
from jax.experimental import pallas as pl
from jax.experimental.pallas import tpu as pltpu
from jax.sharding import PartitionSpec as P

PTS = 8
ROWS = 128
BLOCKS_PER_STEP = 8

NODES = [
    float(v)
    for v in np.cos(
        np.float32(math.pi) * (np.float32(2.0) * np.arange(PTS, dtype=np.float32) + np.float32(1.0)) / np.float32(2.0 * PTS)
    ).astype(np.float32)
]


def from_partner(shard, axis, apart):
    return lax.ppermute(shard, axis, [(i, i ^ 1 << apart) for i in range(lax.axis_size(axis))])


def swapped(block):
    half = block.shape[-1] // 2
    return jnp.concatenate([-block[..., half:], block[..., :half]], axis=-1)


def apply_map(weights, block):
    return jnp.einsum("jk,...kc->...jc", weights, block, preferred_element_type=jnp.float32)


def mix(block, other, weights):
    plain = apply_map(weights[0, 0], block) + apply_map(weights[1, 0], other)
    turned = apply_map(weights[0, 1], block) + apply_map(weights[1, 1], other)
    return (plain + swapped(turned)).astype(jnp.bfloat16)


def basis(u, row):
    ub = jnp.broadcast_to(u, (PTS, ROWS))
    tcol = jnp.zeros((PTS, ROWS), jnp.float32)
    for j in range(PTS):
        tcol = jnp.where(row == j, NODES[j], tcol)
    term = jnp.ones((PTS, ROWS), jnp.float32)
    for m in range(PTS):
        own = row == m
        num = jnp.where(own, 1.0, ub - NODES[m])
        den = jnp.where(own, 1.0, tcol - NODES[m])
        term = term * num / den
    return term


def sample_kernel(leaf_ref, count_ref, pos_ref, grid_ref, out_ref):
    step = pl.program_id(0)
    row = lax.broadcasted_iota(jnp.int32, (PTS, ROWS), 0)
    live_row = lax.broadcasted_iota(jnp.int32, (ROWS, out_ref.shape[1]), 0)
    for i in range(BLOCKS_PER_STEP):
        b = step * BLOCKS_PER_STEP + i
        u = pos_ref[:, i * ROWS:(i + 1) * ROWS]
        lx = basis(u[0:1, :], row)
        ly = basis(u[1:2, :], row)
        lz = basis(u[2:3, :], row)
        pieces = []
        for jx in range(PTS):
            bx = jnp.broadcast_to(lx[jx:jx + 1, :], (PTS, ROWS))
            for jy in range(PTS):
                by = jnp.broadcast_to(ly[jy:jy + 1, :], (PTS, ROWS))
                pieces.append((bx * by) * lz)
        weights_t = jnp.concatenate(pieces, axis=0).astype(jnp.bfloat16)
        leaf = leaf_ref[b]
        place = ((leaf // 2) % 4) * 4 + (leaf // 8) * 2 + leaf % 2
        values = jnp.dot(grid_ref[place], weights_t, preferred_element_type=jnp.float32).T
        values = jnp.where(live_row < count_ref[b], values, 0.0)
        out_ref[i * ROWS:(i + 1) * ROWS, :] = values.astype(out_ref.dtype)


def sample(grid, positions, block_leaf, block_count):
    lx, ly, lz, cheb, cols = grid.shape
    leaf_grid = jnp.transpose(grid, (1, 0, 2, 4, 3)).reshape(ly * lx * lz, cols, cheb)
    blocks = block_leaf.shape[0]
    width = BLOCKS_PER_STEP * ROWS
    spec = pltpu.PrefetchScalarGridSpec(
        num_scalar_prefetch=2,
        grid=(blocks // BLOCKS_PER_STEP,),
        in_specs=[
            pl.BlockSpec((3, width), lambda s, lf, ct: (0, s)),
            pl.BlockSpec((lx * ly * lz, cols, cheb), lambda s, lf, ct: (0, 0, 0)),
        ],
        out_specs=pl.BlockSpec((width, cols), lambda s, lf, ct: (s, 0)),
    )
    return pl.pallas_call(
        sample_kernel,
        grid_spec=spec,
        out_shape=jax.ShapeDtypeStruct((blocks * ROWS, cols), jnp.bfloat16),
    )(block_leaf, block_count, positions, leaf_grid)


LEVEL_PLAN = (("gx", 0), ("gx", 1), ("gy", 0), ("gz", 0))


def pipelined(coefficients, level_weights, chunks):
    cells = [coefficients[:, k:k + 1] for k in range(chunks)]
    levels = len(LEVEL_PLAN)
    for tick in range(chunks + levels - 1):
        active = [k for k in range(chunks) if 0 <= tick - k < levels]
        ready = {}
        for k in active:
            if k > 0 and tick - k + 1 < levels:
                ready[k], _ = lax.optimization_barrier((cells[k], cells[k - 1]))
            else:
                ready[k] = cells[k]
        for k in active:
            level = tick - k
            axis, bit = LEVEL_PLAN[level]
            block = ready[k]
            other = from_partner(block, axis, bit)
            cells[k] = mix(block, other, level_weights[level])
    return cells


def from_below(slab, axis):
    count = lax.axis_size(axis)
    return lax.ppermute(slab, axis, [(i, i + 1) for i in range(count - 1)])


def from_above(slab, axis):
    count = lax.axis_size(axis)
    return lax.ppermute(slab, axis, [(i + 1, i) for i in range(count - 1)])


def faces(cells, axis, dim):
    size = cells.shape[dim]
    first = lax.slice_in_dim(cells, 0, 1, axis=dim)
    last = lax.slice_in_dim(cells, size - 1, size, axis=dim)
    below = jnp.concatenate([from_below(last, axis), lax.slice_in_dim(cells, 0, size - 1, axis=dim)], axis=dim)
    above = jnp.concatenate([lax.slice_in_dim(cells, 1, size, axis=dim), from_above(first, axis)], axis=dim)
    return below, above


def local(coefficients, level_weights, coupling, positions, block_leaf, block_count):
    chunks = coefficients.shape[1]
    cells = jnp.concatenate(pipelined(coefficients, level_weights, chunks), axis=1)
    minus_z, plus_z = faces(cells, "gz", 2)
    minus_x, plus_x = faces(cells, "gx", 0)
    size = cells.shape[1]
    below_y = from_below(cells[:, size - 1:], "gy")
    minus_y = jnp.concatenate([below_y, cells[:, :size - 1]], axis=1)
    plus_y = jnp.concatenate([cells[:, 1:], from_above(cells[:, :1], "gy")], axis=1)
    neighbours = (minus_x, plus_x, minus_y, plus_y, minus_z, plus_z)
    total = cells.astype(jnp.float32)
    for index in range(6):
        total = total + apply_map(coupling[index], neighbours[index])
    grid = total.astype(jnp.bfloat16)
    return sample(grid, positions, block_leaf, block_count)


def solution(mesh):
    placed = (
        P("gx", "gy", "gz", None, None),
        P(),
        P(),
        P(None, ("gx", "gy", "gz")),
        P(("gx", "gy", "gz")),
        P(("gx", "gy", "gz")),
    )

    return jax.shard_map(local, mesh=mesh, in_specs=placed, out_specs=P(("gx", "gy", "gz"), None), check_vma=False)
```
